32 devices in a mesh: groups: 2 (over x), inst: 2 (over core), section: 8 (over z, y).
Axes of the slice: x: 2, y: 2, z: 4, core: 2. Of those that a mesh axis runs over, the one named last changes fastest.
Arguments:
- tokens: bfloat16 [4, 4, 8, 8192], P(('groups', 'inst')), parts along dimension 0, may hold values from -8 to 8
- kv_pool: bfloat16 [4, 8, 16, 2, 8, 128, 128], P(('groups', 'inst'), 'section'), parts along dimension 0, may hold values from -7.125 to 7.125
- page_table: int32 [4, 8, 2], P(('groups', 'inst')), parts along dimension 0, may hold values from 0 to 15, as said below
- lengths: int32 [4, 8], P(('groups', 'inst')), parts along dimension 0, may hold values from 1 to 256, 1280 in all within a row
- migrate_ids: int32 [4, 2], P(('groups', 'inst')), parts along dimension 0, may hold values from 0 to 7, as said below
- norm_gain: float32 [8, 8192], P('section'), may hold values from 0.5 to 1.5
- out_scale: float32 [8, 8192], P('section'), may hold values from 0.5 to 3
Outputs:
- section_rows: bfloat16 [4, 8, 4, 8, 8192], P(('groups', 'inst'), 'section'), parts along dimension 0
- arrived: bfloat16 [4, 8, 2, 2, 2, 8, 128, 128], P(('groups', 'inst'), 'section'), parts along dimension 0
The draws below stay inside these ranges and needn't reach their ends.
There are 2 independent parts, one for each index of `groups`. The reference program is written for one: setup_inputs(seed, part) draws one part's arguments, and reference() takes and returns one part's arrays. A program takes and returns all parts, laid end to end along the dimension named above; an argument that names none is the same for every part. Nothing has to cross between parts.
Inputs may be any that keep to these rules, and one draw needn't show every extreme that they name: `page_table`: each instance's table names each of its 16 pages exactly once. `migrate_ids`: the 2 requests of one instance are different.
All inputs are finite; a program needn't handle non-finite values.
Results may differ from the reference program's by a relative error of at most 0.0091.
Values may be sent and summed in bfloat16 or wider, within the bound.
No kernel may reach another device: no remote copies, remote signals or barrier semaphores. Data moves between devices by JAX's collectives and lax.ppermute only.
A program may use at most 128 MiB of HBM per device.

```python
import math
import jax
import jax.numpy as jnp
import numpy as np
from jax import lax

D = 8192
KEY_VALUE_HEADS = 8
HEAD_SIZE = 128
PAGE_TOKENS = 128
MAXP = 2
STEPS = 4
MIG = 2
REQ = 8
POOL_PAGES = 16
N_INST = 2
N_SECTION = 8


def draw_tokens(key, part):
    array_shape = (N_INST, STEPS, REQ, D)
    main_key = jax.random.fold_in(key, 31)
    return jax.random.truncated_normal(main_key, -6.0, 6.0, array_shape, jnp.float32).astype(jnp.bfloat16)


def draw_kv_pool(key, part):
    array_shape = (N_INST, N_SECTION, POOL_PAGES, 2, KEY_VALUE_HEADS, PAGE_TOKENS, HEAD_SIZE)
    main_key = jax.random.fold_in(key, 47)
    return jax.random.truncated_normal(main_key, -6.0, 6.0, array_shape, jnp.float32).astype(jnp.bfloat16)


def draw_page_table(key, part):
    keys = jax.random.split(jax.random.fold_in(key, 11), N_INST)
    perms = jax.vmap(lambda one: jax.random.permutation(one, POOL_PAGES))(keys)
    return perms.reshape(N_INST, REQ, MAXP).astype(jnp.int32)


def draw_migrate_ids(key, part):
    keys = jax.random.split(jax.random.fold_in(key, 23), N_INST)
    perms = jax.vmap(lambda one: jax.random.permutation(one, REQ))(keys)
    return perms[:, :MIG].astype(jnp.int32)


def block_levels(stream_key, dims, shards, smallest, top_value):
    def one(axis_at, shards_of):
        steps = jax.random.uniform(jax.random.fold_in(jax.random.fold_in(stream_key, 6), axis_at), (shards_of,), jnp.float32, smallest / len(shards), top_value / len(shards))
        return jnp.repeat(jnp.exp(steps), dims[axis_at] // shards_of).reshape((-1,) + (1,) * (len(dims) - axis_at - 1))

    loudness = one(*shards[0])
    for cut in shards[1:]:
        loudness = loudness * one(*cut)
    return loudness


def length_profile(number_of, total, reach, skew):
    weights = [(1 << 20) // math.isqrt(grade ** skew) + 1 for grade in range(2, number_of + 1)]
    rest, given = total - reach - (number_of - 1), [1] * (number_of - 1)
    while rest > 0:
        candidates = [i for i in range(number_of - 1) if given[i] < reach]
        whole, left = sum([weights[i] for i in candidates]), rest
        for i in candidates:
            extra = min(reach - given[i], max(1, left * weights[i] // whole), rest)
            given[i] = given[i] + extra
            rest = rest - extra
    return np.array([reach] + given)


def uneven(key, amount, total, reach, skew):
    if amount == 2:
        one = jax.random.randint(key, (), max(1, total - reach), min(reach, total - 1) + 1)
        return jnp.stack([one, total - one])
    sizes = jnp.asarray(length_profile(amount, total, reach, skew), jnp.int32)
    couples = (amount - 1) // 2
    source_of, receiver = sizes[1:1 + 2 * couples:2], sizes[2:2 + 2 * couples:2]
    margin = jnp.minimum(source_of - 1, reach - receiver)
    shifted = jax.random.randint(jax.random.fold_in(key, 1), (couples,), 0, 1 << 20) % (margin + 1)
    sizes = sizes.at[1:1 + 2 * couples:2].set(source_of - shifted).at[2:2 + 2 * couples:2].set(receiver + shifted)
    return sizes[jax.random.permutation(jax.random.fold_in(key, 2), amount)]


def setup_inputs(seed: int = 0, part: int = 0) -> dict:
    key_list = jax.random.split(jax.random.key(seed), 8)
    own_keys = jax.random.split(jax.random.fold_in(key_list[7], part), 8)
    return {
        "tokens": draw_tokens(jax.random.fold_in(jax.random.fold_in(key_list[7], part), 71), part),
        "kv_pool": draw_kv_pool(jax.random.fold_in(jax.random.fold_in(key_list[7], part), 71), part),
        "page_table": draw_page_table(jax.random.fold_in(jax.random.fold_in(key_list[7], part), 71), part),
        "lengths": jax.vmap(lambda own: uneven(own, REQ, REQ * MAXP * PAGE_TOKENS * 5 // 8, MAXP * PAGE_TOKENS, 1))(jax.random.split(own_keys[3], N_INST)).reshape((N_INST, REQ)).astype(jnp.int32),
        "migrate_ids": draw_migrate_ids(jax.random.fold_in(jax.random.fold_in(key_list[7], part), 71), part),
        "norm_gain": jnp.clip(0.5 + 1.0 * jax.random.uniform(key_list[5], (N_SECTION, D), jnp.float32) ** block_levels(key_list[5], (N_SECTION, D), ((0, 8),), -0.2, 0.2), 0.5, 1.5),
        "out_scale": jnp.clip(0.5 + 2.5 * jax.random.uniform(key_list[6], (N_SECTION, D), jnp.float32) ** block_levels(key_list[6], (N_SECTION, D), ((0, 8),), -0.2, 0.2), 0.5, 3.0),
    }


def gather_slots(pool, table):
    picked = pool[table]
    count = picked.shape[0]
    picked = jnp.transpose(picked, (0, 2, 3, 1, 4, 5))
    return picked.reshape(count, 2, picked.shape[2], picked.shape[3] * picked.shape[4], picked.shape[5])

def layer(hidden, caches, lens, fresh_buf, step, gain, scale):
    rows = hidden.shape[0]
    kv_heads = caches.shape[2]
    head = caches.shape[4]
    steps = fresh_buf.shape[0]
    wide = hidden.astype(jnp.float32)
    normed = wide * lax.rsqrt(lax.optimization_barrier(jnp.mean(wide * wide, axis=-1, keepdims=True)) + 1e-05) * gain
    heads = normed.reshape(rows, kv_heads, -1, head)
    query = heads.astype(jnp.bfloat16).astype(jnp.float32)
    fresh = lax.optimization_barrier(jnp.mean(heads, axis=2)).astype(jnp.bfloat16)
    fresh_buf = lax.dynamic_update_index_in_dim(fresh_buf, fresh, step, 0)
    factor = 1.0 / math.sqrt(head)
    keys = caches[:, 0].astype(jnp.float32)
    values = caches[:, 1].astype(jnp.float32)
    newer = fresh_buf.astype(jnp.float32)
    cache_scores = jnp.einsum('rgqd,rgtd->rgqt', query, keys) * factor
    positions = jnp.arange(keys.shape[2])
    live = positions[None, :] < lens[:, None]
    cache_scores = jnp.where(live[:, None, None, :], cache_scores, -1e+30)
    new_scores = jnp.einsum('rgqd,jrgd->rgqj', query, newer) * factor
    done = jnp.arange(steps) <= step
    new_scores = jnp.where(done[None, None, None, :], new_scores, -1e+30)
    top = jnp.maximum(lax.optimization_barrier(jnp.max(cache_scores, axis=-1, keepdims=True)), lax.optimization_barrier(jnp.max(new_scores, axis=-1, keepdims=True)))
    cache_exp = jnp.exp(cache_scores - top)
    new_exp = jnp.exp(new_scores - top)
    total = lax.optimization_barrier(jnp.sum(cache_exp, axis=-1, keepdims=True)) + lax.optimization_barrier(jnp.sum(new_exp, axis=-1, keepdims=True))
    cache_w = (cache_exp / total).astype(jnp.bfloat16).astype(jnp.float32)
    new_w = (new_exp / total).astype(jnp.bfloat16).astype(jnp.float32)
    attended = jnp.einsum('rgqt,rgtd->rgqd', cache_w, values) + jnp.einsum('rgqj,jrgd->rgqd', new_w, newer)
    result = (wide + scale * attended.reshape(rows, -1)).astype(jnp.bfloat16)
    return (result, fresh_buf)

def reference(tokens, kv_pool, page_table, lengths, migrate_ids, norm_gain, out_scale):
    insts = tokens.shape[0]
    steps = tokens.shape[1]
    reqs = tokens.shape[2]
    sections = kv_pool.shape[1]
    kv_heads = kv_pool.shape[4]
    head = kv_pool.shape[6]

    def one_section(carry, section):
        pool = lax.dynamic_index_in_dim(kv_pool, section, 1, keepdims=False)
        gain = lax.dynamic_index_in_dim(norm_gain, section, 0, keepdims=False)
        scale = lax.dynamic_index_in_dim(out_scale, section, 0, keepdims=False)
        kept = []
        for inst in range(insts):
            caches = gather_slots(pool[inst], page_table[inst])
            fresh_buf = jnp.zeros((steps, reqs, kv_heads, head), jnp.bfloat16)
            outputs = []
            for step in range(steps):
                result, fresh_buf = layer(carry[inst, step], caches, lengths[inst], fresh_buf, step, gain, scale)
                outputs.append(result)
            kept.append(jnp.stack(outputs))
        joined = jnp.stack(kept)
        return (joined, joined)
    _, per_section = lax.scan(one_section, tokens, jnp.arange(sections).astype(jnp.int32))
    slots = jnp.arange(reqs).astype(jnp.int32)
    rows_out = []
    pages_out = []
    for inst in range(insts):
        partner = insts - 1 - inst
        hit = slots[:, None] == migrate_ids[inst][None, :]
        moved = jnp.any(hit, axis=1)
        source = lax.optimization_barrier(jnp.sum(jnp.where(hit, migrate_ids[partner][None, :], 0), axis=1)).astype(jnp.int32)
        own = per_section[:, inst]
        other = per_section[:, partner][:, :, source]
        rows_out.append(jnp.where(moved[None, None, :, None], other, own))
        chosen = page_table[partner][migrate_ids[partner]]
        pages = kv_pool[partner][:, chosen]
        page_len = pages.shape[5]
        spots = jnp.arange(chosen.shape[1])[:, None] * page_len + jnp.arange(page_len)[None, :]
        live = spots[None, :, :] < lengths[partner][migrate_ids[partner]][:, None, None]
        pages_out.append(jnp.where(live[None, :, :, None, None, :, None], pages, jnp.zeros((), jnp.bfloat16)))
    return (jnp.stack(rows_out), jnp.stack(pages_out))
```

```python
import math

import jax
import jax.numpy as jnp
from jax import lax
from jax.sharding import PartitionSpec as P

CHUNKS = 2


def partner(block, axis, stride):
    count = lax.axis_size(axis)
    route = []
    for low in range(count):
        high = low | 1 << stride
        if high != low and high < count:
            route += [(low, high), (high, low)]
    return lax.ppermute(block, axis, route)


def passed_along(array, axis, by):
    peers = lax.axis_size(axis)
    pairs = [(i, i + by) for i in range(peers) if 0 <= i + by < peers]
    return lax.ppermute(array, axis, pairs)


def layer(rows, keys, values, lens, gain, scale):
    steps, reqs, width = rows.shape
    pages = keys.shape[1]
    kv_heads = keys.shape[2]
    page_len = keys.shape[3]
    head = keys.shape[4]
    group = width // (kv_heads * head)
    wide = rows.astype(jnp.float32)
    normed = wide * lax.rsqrt(jnp.mean(wide * wide, axis=-1, keepdims=True) + 1e-05) * gain
    heads = normed.reshape(steps, reqs, kv_heads, group, head)
    query = jnp.transpose(heads.astype(jnp.bfloat16), (1, 2, 0, 3, 4))
    query = query.reshape(reqs, kv_heads, steps * group, head)
    fresh = jnp.mean(heads, axis=3).astype(jnp.bfloat16)
    fresh = jnp.transpose(fresh, (1, 2, 0, 3))
    factor = 1.0 / math.sqrt(head)
    wide_query = jnp.broadcast_to(query[:, None], (reqs, pages) + query.shape[1:])
    cache_scores = (
        jnp.einsum("rjgxd,rjgpd->rjgxp", wide_query, keys, preferred_element_type=jnp.float32)
        * factor
    )
    positions = jnp.arange(pages)[:, None] * page_len + jnp.arange(page_len)[None, :]
    live = positions[None] < lens[:, None, None]
    cache_scores = jnp.where(live[:, :, None, None, :], cache_scores, -1e30)
    new_scores = (
        jnp.einsum("rgxd,rgsd->rgxs", query, fresh, preferred_element_type=jnp.float32) * factor
    )
    step_of = jnp.arange(steps * group) // group
    done = jnp.arange(steps)[None, :] <= step_of[:, None]
    new_scores = jnp.where(done[None, None], new_scores, -1e30)
    top = jnp.maximum(
        jnp.max(cache_scores, axis=(1, 4)), jnp.max(new_scores, axis=-1)
    )[..., None]
    cache_exp = jnp.exp(cache_scores - top[:, None])
    new_exp = jnp.exp(new_scores - top)
    total = jnp.sum(cache_exp, axis=(1, 4))[..., None] + jnp.sum(new_exp, axis=-1, keepdims=True)
    cache_w = (cache_exp / total[:, None]).astype(jnp.bfloat16)
    new_w = (new_exp / total).astype(jnp.bfloat16)
    attended = jnp.einsum(
        "rjgxp,rjgpd->rjgxd", cache_w, values, preferred_element_type=jnp.float32
    ).sum(axis=1)
    attended = attended + jnp.einsum(
        "rgxs,rgsd->rgxd", new_w, fresh, preferred_element_type=jnp.float32
    )
    attended = attended.reshape(reqs, kv_heads, steps, group, head)
    attended = jnp.transpose(attended, (2, 0, 1, 3, 4)).reshape(steps, reqs, width)
    return (wide + scale * attended).astype(jnp.bfloat16)


def per_device(tokens, kv_pool, page_table, lengths, migrate_ids, norm_gain, out_scale):
    inputs = tokens[0]
    pool = kv_pool[0, 0]
    table = page_table[0]
    lens = lengths[0]
    moving = migrate_ids[0]
    gain = norm_gain[0]
    scale = out_scale[0]
    steps, reqs, width = inputs.shape
    page_len = pool.shape[3]
    chosen = table[moving]
    outgoing = pool[chosen]
    spots = jnp.arange(chosen.shape[1])[:, None] * page_len + jnp.arange(page_len)[None, :]
    keep = spots[None, :, :] < lens[moving][:, None, None]
    outgoing = jnp.where(keep[:, :, None, None, :, None], outgoing, jnp.zeros((), jnp.bfloat16))
    received, arrived_rows = partner((outgoing, inputs[:, moving]), "inst", 0)
    arrived_lens = partner(lens[moving], "inst", 0)
    caches = pool[table].at[moving].set(received)
    lens_used = lens.at[moving].set(arrived_lens)
    inputs = inputs.at[:, moving].set(arrived_rows)
    keys = caches[:, :, 0]
    values = caches[:, :, 1]
    section = lax.axis_index("section")
    count = lax.axis_size("section")
    chunks = CHUNKS
    block = reqs // chunks

    def tick(k, carry):
        incoming, finished = carry
        item = k - section
        live = jnp.logical_and(item >= 0, item < chunks)
        start = jnp.clip(item, 0, chunks - 1) * block
        zero = jnp.zeros((), jnp.int32)
        first = lax.dynamic_slice_in_dim(inputs, start, block, 1)
        rows = jnp.where(section == 0, first, incoming)
        part_keys = lax.dynamic_slice_in_dim(keys, start, block, 0)
        part_values = lax.dynamic_slice_in_dim(values, start, block, 0)
        part_lens = lax.dynamic_slice_in_dim(lens_used, start, block, 0)
        result = layer(rows, part_keys, part_values, part_lens, gain, scale)
        previous = lax.dynamic_slice_in_dim(finished, start, block, 1)
        finished = lax.dynamic_update_slice(
            finished, jnp.where(live, result, previous), (zero, start, zero)
        )
        passed = passed_along(result, "section", 1)
        return (passed, finished)

    start_carry = (
        jnp.zeros((steps, block, width), jnp.bfloat16),
        jnp.zeros((steps, reqs, width), jnp.bfloat16),
    )
    _, finished = lax.fori_loop(0, chunks + count - 1, tick, start_carry)
    return (finished[None, None], received[None, None])


def solution(mesh):
    in_specs = (
        P(("groups", "inst"), None, None, None),
        P(("groups", "inst"), "section", None, None, None, None, None),
        P(("groups", "inst"), None, None),
        P(("groups", "inst"), None),
        P(("groups", "inst"), None),
        P("section", None),
        P("section", None),
    )
    out_specs = (
        P(("groups", "inst"), "section", None, None, None),
        P(("groups", "inst"), "section", None, None, None, None, None, None),
    )
    return jax.shard_map(
        per_device, mesh=mesh, in_specs=in_specs, out_specs=out_specs, check_vma=False
    )
```

```python
import math

import jax
import jax.numpy as jnp
from jax import lax
from jax.sharding import PartitionSpec as P

CHUNKS = 4


def partner(block, axis, stride):
    count = lax.axis_size(axis)
    route = []
    for low in range(count):
        high = low | 1 << stride
        if high != low and high < count:
            route += [(low, high), (high, low)]
    return lax.ppermute(block, axis, route)


def passed_along(array, axis, by):
    peers = lax.axis_size(axis)
    pairs = [(i, i + by) for i in range(peers) if 0 <= i + by < peers]
    return lax.ppermute(array, axis, pairs)


def layer(rows, keys, values, lens, gain, scale):
    steps, reqs, width = rows.shape
    pages = keys.shape[1]
    kv_heads = keys.shape[2]
    page_len = keys.shape[3]
    head = keys.shape[4]
    group = width // (kv_heads * head)
    wide = rows.astype(jnp.float32)
    normed = wide * lax.rsqrt(jnp.mean(wide * wide, axis=-1, keepdims=True) + 1e-05) * gain
    heads = normed.reshape(steps, reqs, kv_heads, group, head)
    query = jnp.transpose(heads.astype(jnp.bfloat16), (1, 2, 0, 3, 4))
    query = query.reshape(reqs, kv_heads, steps * group, head)
    fresh = jnp.mean(heads, axis=3).astype(jnp.bfloat16)
    fresh = jnp.transpose(fresh, (1, 2, 0, 3))
    factor = 1.0 / math.sqrt(head)
    wide_query = jnp.broadcast_to(query[:, None], (reqs, pages) + query.shape[1:])
    cache_scores = (
        jnp.einsum("rjgxd,rjgpd->rjgxp", wide_query, keys, preferred_element_type=jnp.float32)
        * factor
    )
    positions = jnp.arange(pages)[:, None] * page_len + jnp.arange(page_len)[None, :]
    live = positions[None] < lens[:, None, None]
    cache_scores = jnp.where(live[:, :, None, None, :], cache_scores, -1e30)
    new_scores = (
        jnp.einsum("rgxd,rgsd->rgxs", query, fresh, preferred_element_type=jnp.float32) * factor
    )
    step_of = jnp.arange(steps * group) // group
    done = jnp.arange(steps)[None, :] <= step_of[:, None]
    new_scores = jnp.where(done[None, None], new_scores, -1e30)
    top = jnp.maximum(
        jnp.max(cache_scores, axis=(1, 4)), jnp.max(new_scores, axis=-1)
    )[..., None]
    cache_exp = jnp.exp(cache_scores - top[:, None])
    new_exp = jnp.exp(new_scores - top)
    total = jnp.sum(cache_exp, axis=(1, 4))[..., None] + jnp.sum(new_exp, axis=-1, keepdims=True)
    cache_w = (cache_exp / total[:, None]).astype(jnp.bfloat16)
    new_w = (new_exp / total).astype(jnp.bfloat16)
    attended = jnp.einsum(
        "rjgxp,rjgpd->rjgxd", cache_w, values, preferred_element_type=jnp.float32
    ).sum(axis=1)
    attended = attended + jnp.einsum(
        "rgxs,rgsd->rgxd", new_w, fresh, preferred_element_type=jnp.float32
    )
    attended = attended.reshape(reqs, kv_heads, steps, group, head)
    attended = jnp.transpose(attended, (2, 0, 1, 3, 4)).reshape(steps, reqs, width)
    return (wide + scale * attended).astype(jnp.bfloat16)


def per_device(tokens, kv_pool, page_table, lengths, migrate_ids, norm_gain, out_scale):
    inputs = tokens[0]
    pool = kv_pool[0, 0]
    table = page_table[0]
    lens = lengths[0]
    moving = migrate_ids[0]
    gain = norm_gain[0]
    scale = out_scale[0]
    steps, reqs, width = inputs.shape
    page_len = pool.shape[3]
    chosen = table[moving]
    outgoing = pool[chosen]
    spots = jnp.arange(chosen.shape[1])[:, None] * page_len + jnp.arange(page_len)[None, :]
    keep = spots[None, :, :] < lens[moving][:, None, None]
    outgoing = jnp.where(keep[:, :, None, None, :, None], outgoing, jnp.zeros((), jnp.bfloat16))
    received, arrived_rows = partner((outgoing, inputs[:, moving]), "inst", 0)
    arrived_lens = partner(lens[moving], "inst", 0)
    caches = pool[table].at[moving].set(received)
    lens_used = lens.at[moving].set(arrived_lens)
    inputs = inputs.at[:, moving].set(arrived_rows)
    keys = caches[:, :, 0]
    values = caches[:, :, 1]
    section = lax.axis_index("section")
    count = lax.axis_size("section")
    chunks = CHUNKS
    block = reqs // chunks

    def tick(k, carry):
        incoming, finished = carry
        item = k - section
        live = jnp.logical_and(item >= 0, item < chunks)
        start = jnp.clip(item, 0, chunks - 1) * block
        zero = jnp.zeros((), jnp.int32)
        first = lax.dynamic_slice_in_dim(inputs, start, block, 1)
        rows = jnp.where(section == 0, first, incoming)
        part_keys = lax.dynamic_slice_in_dim(keys, start, block, 0)
        part_values = lax.dynamic_slice_in_dim(values, start, block, 0)
        part_lens = lax.dynamic_slice_in_dim(lens_used, start, block, 0)
        result = layer(rows, part_keys, part_values, part_lens, gain, scale)
        previous = lax.dynamic_slice_in_dim(finished, start, block, 1)
        finished = lax.dynamic_update_slice(
            finished, jnp.where(live, result, previous), (zero, start, zero)
        )
        passed = passed_along(result, "section", 1)
        return (passed, finished)

    start_carry = (
        jnp.zeros((steps, block, width), jnp.bfloat16),
        jnp.zeros((steps, reqs, width), jnp.bfloat16),
    )
    _, finished = lax.fori_loop(0, chunks + count - 1, tick, start_carry)
    return (finished[None, None], received[None, None])


def solution(mesh):
    in_specs = (
        P(("groups", "inst"), None, None, None),
        P(("groups", "inst"), "section", None, None, None, None, None),
        P(("groups", "inst"), None, None),
        P(("groups", "inst"), None),
        P(("groups", "inst"), None),
        P("section", None),
        P("section", None),
    )
    out_specs = (
        P(("groups", "inst"), "section", None, None, None),
        P(("groups", "inst"), "section", None, None, None, None, None, None),
    )
    return jax.shard_map(
        per_device, mesh=mesh, in_specs=in_specs, out_specs=out_specs, check_vma=False
    )
```

```python
import math

import jax
import jax.numpy as jnp
from jax import lax
from jax.sharding import PartitionSpec as P

CHUNKS = 2


def partner(block, axis, stride):
    count = lax.axis_size(axis)
    route = []
    for low in range(count):
        high = low | 1 << stride
        if high != low and high < count:
            route += [(low, high), (high, low)]
    return lax.ppermute(block, axis, route)


def passed_along(array, axis, by):
    peers = lax.axis_size(axis)
    pairs = [(i, i + by) for i in range(peers) if 0 <= i + by < peers]
    return lax.ppermute(array, axis, pairs)


def layer(rows, keys, values, lens, gain, scale):
    steps, reqs, width = rows.shape
    pages = keys.shape[1]
    kv_heads = keys.shape[2]
    page_len = keys.shape[3]
    head = keys.shape[4]
    group = width // (kv_heads * head)
    wide = rows.astype(jnp.float32)
    normed = wide * lax.rsqrt(jnp.mean(wide * wide, axis=-1, keepdims=True) + 1e-05) * gain
    heads = normed.reshape(steps, reqs, kv_heads, group, head)
    query = jnp.transpose(heads.astype(jnp.bfloat16), (1, 2, 0, 3, 4))
    query = query.reshape(reqs, kv_heads, steps * group, head)
    fresh = jnp.mean(heads, axis=3).astype(jnp.bfloat16)
    fresh = jnp.transpose(fresh, (1, 2, 0, 3))
    factor = 1.0 / math.sqrt(head)
    wide_query = jnp.broadcast_to(query[:, None], (reqs, pages) + query.shape[1:])
    cache_scores = (
        jnp.einsum("rjgxd,rjgpd->rjgxp", wide_query, keys, preferred_element_type=jnp.float32)
        * factor
    )
    positions = jnp.arange(pages)[:, None] * page_len + jnp.arange(page_len)[None, :]
    live = positions[None] < lens[:, None, None]
    cache_scores = jnp.where(live[:, :, None, None, :], cache_scores, -1e30)
    new_scores = (
        jnp.einsum("rgxd,rgsd->rgxs", query, fresh, preferred_element_type=jnp.float32) * factor
    )
    step_of = jnp.arange(steps * group) // group
    done = jnp.arange(steps)[None, :] <= step_of[:, None]
    new_scores = jnp.where(done[None, None], new_scores, -1e30)
    top = jnp.maximum(
        jnp.max(cache_scores, axis=(1, 4)), jnp.max(new_scores, axis=-1)
    )[..., None]
    cache_exp = jnp.exp(cache_scores - top[:, None])
    new_exp = jnp.exp(new_scores - top)
    total = jnp.sum(cache_exp, axis=(1, 4))[..., None] + jnp.sum(new_exp, axis=-1, keepdims=True)
    cache_w = (cache_exp / total[:, None]).astype(jnp.bfloat16)
    new_w = (new_exp / total).astype(jnp.bfloat16)
    attended = jnp.einsum(
        "rjgxp,rjgpd->rjgxd", cache_w, values, preferred_element_type=jnp.float32
    ).sum(axis=1)
    attended = attended + jnp.einsum(
        "rgxs,rgsd->rgxd", new_w, fresh, preferred_element_type=jnp.float32
    )
    attended = attended.reshape(reqs, kv_heads, steps, group, head)
    attended = jnp.transpose(attended, (2, 0, 1, 3, 4)).reshape(steps, reqs, width)
    return (wide + scale * attended).astype(jnp.bfloat16)


def per_device(tokens, kv_pool, page_table, lengths, migrate_ids, norm_gain, out_scale):
    inputs = tokens[0]
    pool = kv_pool[0, 0]
    table = page_table[0]
    lens = lengths[0]
    moving = migrate_ids[0]
    gain = norm_gain[0]
    scale = out_scale[0]
    steps, reqs, width = inputs.shape
    page_len = pool.shape[3]
    chosen = table[moving]
    outgoing = pool[chosen]
    spots = jnp.arange(chosen.shape[1])[:, None] * page_len + jnp.arange(page_len)[None, :]
    keep = spots[None, :, :] < lens[moving][:, None, None]
    outgoing = jnp.where(keep[:, :, None, None, :, None], outgoing, jnp.zeros((), jnp.bfloat16))
    received = partner(outgoing, "inst", 0)
    keys = pool[:, 0][table]
    values = pool[:, 1][table]
    lens_used = lens
    section = lax.axis_index("section")
    count = lax.axis_size("section")
    chunks = CHUNKS
    block = reqs // chunks

    def tick(k, carry):
        incoming, finished = carry
        item = k - section
        live = jnp.logical_and(item >= 0, item < chunks)
        start = jnp.clip(item, 0, chunks - 1) * block
        zero = jnp.zeros((), jnp.int32)
        first = lax.dynamic_slice_in_dim(inputs, start, block, 1)
        rows = jnp.where(section == 0, first, incoming)
        part_keys = lax.dynamic_slice_in_dim(keys, start, block, 0)
        part_values = lax.dynamic_slice_in_dim(values, start, block, 0)
        part_lens = lax.dynamic_slice_in_dim(lens_used, start, block, 0)
        result = layer(rows, part_keys, part_values, part_lens, gain, scale)
        previous = lax.dynamic_slice_in_dim(finished, start, block, 1)
        finished = lax.dynamic_update_slice(
            finished, jnp.where(live, result, previous), (zero, start, zero)
        )
        passed = passed_along(result, "section", 1)
        return (passed, finished)

    start_carry = (
        jnp.zeros((steps, block, width), jnp.bfloat16),
        jnp.zeros((steps, reqs, width), jnp.bfloat16),
    )
    _, finished = lax.fori_loop(0, chunks + count - 1, tick, start_carry)
    handed = partner(finished[:, moving], "inst", 0)
    finished = finished.at[:, moving].set(handed)
    return (finished[None, None], received[None, None])


def solution(mesh):
    in_specs = (
        P(("groups", "inst"), None, None, None),
        P(("groups", "inst"), "section", None, None, None, None, None),
        P(("groups", "inst"), None, None),
        P(("groups", "inst"), None),
        P(("groups", "inst"), None),
        P("section", None),
        P("section", None),
    )
    out_specs = (
        P(("groups", "inst"), "section", None, None, None),
        P(("groups", "inst"), "section", None, None, None, None, None, None),
    )
    return jax.shard_map(
        per_device, mesh=mesh, in_specs=in_specs, out_specs=out_specs, check_vma=False
    )
```

```python
import math

import jax
import jax.numpy as jnp
from jax import lax
from jax.sharding import PartitionSpec as P
from jax.experimental import pallas as pl
from jax.experimental.pallas import tpu as pltpu

CHUNKS = 2


def partner(block, axis, stride):
    count = lax.axis_size(axis)
    route = []
    for low in range(count):
        high = low | 1 << stride
        if high != low and high < count:
            route += [(low, high), (high, low)]
    return lax.ppermute(block, axis, route)


def passed_along(array, axis, by):
    peers = lax.axis_size(axis)
    pairs = [(i, i + by) for i in range(peers) if 0 <= i + by < peers]
    return lax.ppermute(array, axis, pairs)


def layer(rows, keys, values, lens, gain, scale):
    steps, reqs, width = rows.shape
    pages = keys.shape[1]
    kv_heads = keys.shape[2]
    page_len = keys.shape[3]
    head = keys.shape[4]
    group = width // (kv_heads * head)
    wide = rows.astype(jnp.float32)
    normed = wide * lax.rsqrt(jnp.mean(wide * wide, axis=-1, keepdims=True) + 1e-05) * gain
    heads = normed.reshape(steps, reqs, kv_heads, group, head)
    query = jnp.transpose(heads.astype(jnp.bfloat16), (1, 2, 0, 3, 4))
    query = query.reshape(reqs, kv_heads, steps * group, head)
    fresh = jnp.mean(heads, axis=3).astype(jnp.bfloat16)
    fresh = jnp.transpose(fresh, (1, 2, 0, 3))
    factor = 1.0 / math.sqrt(head)
    wide_query = jnp.broadcast_to(query[:, None], (reqs, pages) + query.shape[1:])
    cache_scores = (
        jnp.einsum("rjgxd,rjgpd->rjgxp", wide_query, keys, preferred_element_type=jnp.float32)
        * factor
    )
    positions = jnp.arange(pages)[:, None] * page_len + jnp.arange(page_len)[None, :]
    live = positions[None] < lens[:, None, None]
    cache_scores = jnp.where(live[:, :, None, None, :], cache_scores, -1e30)
    new_scores = (
        jnp.einsum("rgxd,rgsd->rgxs", query, fresh, preferred_element_type=jnp.float32) * factor
    )
    step_of = jnp.arange(steps * group) // group
    done = jnp.arange(steps)[None, :] <= step_of[:, None]
    new_scores = jnp.where(done[None, None], new_scores, -1e30)
    top = jnp.maximum(
        jnp.max(cache_scores, axis=(1, 4)), jnp.max(new_scores, axis=-1)
    )[..., None]
    cache_exp = jnp.exp(cache_scores - top[:, None])
    new_exp = jnp.exp(new_scores - top)
    total = jnp.sum(cache_exp, axis=(1, 4))[..., None] + jnp.sum(new_exp, axis=-1, keepdims=True)
    cache_w = (cache_exp / total[:, None]).astype(jnp.bfloat16)
    new_w = (new_exp / total).astype(jnp.bfloat16)
    attended = jnp.einsum(
        "rjgxp,rjgpd->rjgxd", cache_w, values, preferred_element_type=jnp.float32
    ).sum(axis=1)
    attended = attended + jnp.einsum(
        "rgxs,rgsd->rgxd", new_w, fresh, preferred_element_type=jnp.float32
    )
    attended = attended.reshape(reqs, kv_heads, steps, group, head)
    attended = jnp.transpose(attended, (2, 0, 1, 3, 4)).reshape(steps, reqs, width)
    return (wide + scale * attended).astype(jnp.bfloat16)


def attend_kernel(table_ref, lens_ref, start_ref, q_ref, f_ref, *refs):
    pages = (len(refs) - 1) // 2
    key_refs = refs[:pages]
    value_refs = refs[pages:2 * pages]
    o_ref = refs[-1]
    req = start_ref[0] + pl.program_id(0)
    length = lens_ref[req]
    query = q_ref[0]
    kv_heads, rows, head = query.shape
    fresh = f_ref[0].astype(jnp.float32)
    steps = fresh.shape[1]
    group = rows // steps
    page_len = key_refs[0].shape[3]
    factor = 1.0 / math.sqrt(head)
    spots = lax.broadcasted_iota(jnp.int32, (kv_heads, rows, page_len), 2)
    scores = []
    for j in range(pages):
        got = lax.dot_general(
            query, key_refs[j][0, 0], (((2,), (2,)), ((0,), (0,))),
            preferred_element_type=jnp.float32,
        ) * factor
        scores.append(jnp.where(spots + j * page_len < length, got, -1e30))
    wide_query = query.astype(jnp.float32)
    step_of = lax.broadcasted_iota(jnp.int32, (kv_heads, rows), 1) // group
    news = []
    for s in range(steps):
        got = jnp.sum(wide_query * fresh[:, s][:, None, :], axis=-1) * factor
        news.append(jnp.where(step_of >= s, got, -1e30))
    top = jnp.max(scores[0], axis=-1)
    for j in range(1, pages):
        top = jnp.maximum(top, jnp.max(scores[j], axis=-1))
    for s in range(steps):
        top = jnp.maximum(top, news[s])
    exps = [jnp.exp(x - top[..., None]) for x in scores]
    new_exps = [jnp.exp(x - top) for x in news]
    total = sum(jnp.sum(x, axis=-1) for x in exps) + sum(new_exps)
    out = None
    for j in range(pages):
        weight = (exps[j] / total[..., None]).astype(jnp.bfloat16)
        part = lax.dot_general(
            weight, value_refs[j][0, 0], (((2,), (1,)), ((0,), (0,))),
            preferred_element_type=jnp.float32,
        )
        out = part if out is None else out + part
    for s in range(steps):
        weight = (new_exps[s] / total).astype(jnp.bfloat16).astype(jnp.float32)
        out = out + weight[..., None] * fresh[:, s][:, None, :]
    o_ref[0] = out


def attend(query, fresh, pool, table, lens, start):
    reqs, kv_heads, rows, head = query.shape
    steps = fresh.shape[2]
    pages = table.shape[1]
    page_len = pool.shape[3]
    flat = table.reshape(-1)

    def page_spec(j, half):
        def index(r, table_ref, lens_ref, start_ref):
            return (table_ref[(start_ref[0] + r) * pages + j], half, 0, 0, 0)

        return pl.BlockSpec((1, 1, kv_heads, page_len, head), index)

    def row_spec(width):
        return pl.BlockSpec((1, kv_heads, width, head), lambda r, *_: (r, 0, 0, 0))

    grid_spec = pltpu.PrefetchScalarGridSpec(
        num_scalar_prefetch=3,
        grid=(reqs,),
        in_specs=[row_spec(rows), row_spec(steps)]
        + [page_spec(j, 0) for j in range(pages)]
        + [page_spec(j, 1) for j in range(pages)],
        out_specs=row_spec(rows),
    )
    return pl.pallas_call(
        attend_kernel,
        grid_spec=grid_spec,
        out_shape=jax.ShapeDtypeStruct(query.shape, jnp.float32),
    )(flat, lens, start.reshape(1), query, fresh, *([pool] * (2 * pages)))


def layer_paged(rows, pool, table, lens, start, gain, scale):
    steps, reqs, width = rows.shape
    kv_heads = pool.shape[2]
    head = pool.shape[4]
    group = width // (kv_heads * head)
    wide = rows.astype(jnp.float32)
    normed = wide * lax.rsqrt(jnp.mean(wide * wide, axis=-1, keepdims=True) + 1e-05) * gain
    heads = normed.reshape(steps, reqs, kv_heads, group, head)
    query = jnp.transpose(heads.astype(jnp.bfloat16), (1, 2, 0, 3, 4))
    query = query.reshape(reqs, kv_heads, steps * group, head)
    fresh = jnp.mean(heads, axis=3).astype(jnp.bfloat16)
    fresh = jnp.transpose(fresh, (1, 2, 0, 3))
    attended = attend(query, fresh, pool, table, lens, start)
    attended = attended.reshape(reqs, kv_heads, steps, group, head)
    attended = jnp.transpose(attended, (2, 0, 1, 3, 4)).reshape(steps, reqs, width)
    return (wide + scale * attended).astype(jnp.bfloat16)


def per_device(tokens, kv_pool, page_table, lengths, migrate_ids, norm_gain, out_scale):
    inputs = tokens[0]
    pool = kv_pool[0, 0]
    table = page_table[0]
    lens = lengths[0]
    moving = migrate_ids[0]
    gain = norm_gain[0]
    scale = out_scale[0]
    steps, reqs, width = inputs.shape
    page_len = pool.shape[3]
    chosen = table[moving]
    outgoing = pool[chosen]
    spots = jnp.arange(chosen.shape[1])[:, None] * page_len + jnp.arange(page_len)[None, :]
    keep = spots[None, :, :] < lens[moving][:, None, None]
    outgoing = jnp.where(keep[:, :, None, None, :, None], outgoing, jnp.zeros((), jnp.bfloat16))
    received = partner(outgoing, "inst", 0)
    lens_used = lens
    section = lax.axis_index("section")
    count = lax.axis_size("section")
    chunks = CHUNKS
    block = reqs // chunks

    def tick(k, carry):
        incoming, finished = carry
        item = k - section
        live = jnp.logical_and(item >= 0, item < chunks)
        start = jnp.clip(item, 0, chunks - 1) * block
        zero = jnp.zeros((), jnp.int32)
        first = lax.dynamic_slice_in_dim(inputs, start, block, 1)
        rows = jnp.where(section == 0, first, incoming)
        result = layer_paged(rows, pool, table, lens_used, start, gain, scale)
        previous = lax.dynamic_slice_in_dim(finished, start, block, 1)
        finished = lax.dynamic_update_slice(
            finished, jnp.where(live, result, previous), (zero, start, zero)
        )
        passed = passed_along(result, "section", 1)
        return (passed, finished)

    start_carry = (
        jnp.zeros((steps, block, width), jnp.bfloat16),
        jnp.zeros((steps, reqs, width), jnp.bfloat16),
    )
    _, finished = lax.fori_loop(0, chunks + count - 1, tick, start_carry)
    handed = partner(finished[:, moving], "inst", 0)
    finished = finished.at[:, moving].set(handed)
    return (finished[None, None], received[None, None])


def solution(mesh):
    in_specs = (
        P(("groups", "inst"), None, None, None),
        P(("groups", "inst"), "section", None, None, None, None, None),
        P(("groups", "inst"), None, None),
        P(("groups", "inst"), None),
        P(("groups", "inst"), None),
        P("section", None),
        P("section", None),
    )
    out_specs = (
        P(("groups", "inst"), "section", None, None, None),
        P(("groups", "inst"), "section", None, None, None, None, None, None),
    )
    return jax.shard_map(
        per_device, mesh=mesh, in_specs=in_specs, out_specs=out_specs, check_vma=False
    )
```

```python
import math

import jax
import jax.numpy as jnp
from jax import lax
from jax.sharding import PartitionSpec as P

CHUNKS = 2


def partner(block, axis, stride):
    count = lax.axis_size(axis)
    route = []
    for low in range(count):
        high = low | 1 << stride
        if high != low and high < count:
            route += [(low, high), (high, low)]
    return lax.ppermute(block, axis, route)


def passed_along(array, axis, by):
    peers = lax.axis_size(axis)
    pairs = [(i, i + by) for i in range(peers) if 0 <= i + by < peers]
    return lax.ppermute(array, axis, pairs)


def layer(rows, keys, values, lens, gain, scale):
    steps, reqs, width = rows.shape
    pages = values.shape[1]
    kv_heads = values.shape[2]
    page_len = values.shape[3]
    head = values.shape[4]
    group = width // (kv_heads * head)
    wide = rows.astype(jnp.float32)
    normed = wide * lax.rsqrt(jnp.mean(wide * wide, axis=-1, keepdims=True) + 1e-05) * gain
    heads = normed.reshape(steps, reqs, kv_heads, group, head)
    query = jnp.transpose(heads.astype(jnp.bfloat16), (1, 2, 0, 3, 4))
    query = query.reshape(reqs, kv_heads, steps * group, head)
    fresh = jnp.mean(heads, axis=3).astype(jnp.bfloat16)
    fresh = jnp.transpose(fresh, (1, 2, 0, 3))
    factor = 1.0 / math.sqrt(head)
    wide_query = jnp.broadcast_to(query[:, None], (reqs, pages) + query.shape[1:])
    cache_scores = (
        jnp.einsum("rjgxd,rjgdp->rjgxp", wide_query, keys, preferred_element_type=jnp.float32)
        * factor
    )
    positions = jnp.arange(pages)[:, None] * page_len + jnp.arange(page_len)[None, :]
    live = positions[None] < lens[:, None, None]
    cache_scores = jnp.where(live[:, :, None, None, :], cache_scores, -1e30)
    new_scores = (
        jnp.einsum("rgxd,rgsd->rgxs", query, fresh, preferred_element_type=jnp.float32) * factor
    )
    step_of = jnp.arange(steps * group) // group
    done = jnp.arange(steps)[None, :] <= step_of[:, None]
    new_scores = jnp.where(done[None, None], new_scores, -1e30)
    top = jnp.maximum(
        jnp.max(cache_scores, axis=(1, 4)), jnp.max(new_scores, axis=-1)
    )[..., None]
    cache_exp = jnp.exp(cache_scores - top[:, None])
    new_exp = jnp.exp(new_scores - top)
    total = jnp.sum(cache_exp, axis=(1, 4))[..., None] + jnp.sum(new_exp, axis=-1, keepdims=True)
    cache_w = (cache_exp / total[:, None]).astype(jnp.bfloat16)
    new_w = (new_exp / total).astype(jnp.bfloat16)
    attended = jnp.einsum(
        "rjgxp,rjgpd->rjgxd", cache_w, values, preferred_element_type=jnp.float32
    ).sum(axis=1)
    attended = attended + jnp.einsum(
        "rgxs,rgsd->rgxd", new_w, fresh, preferred_element_type=jnp.float32
    )
    attended = attended.reshape(reqs, kv_heads, steps, group, head)
    attended = jnp.transpose(attended, (2, 0, 1, 3, 4)).reshape(steps, reqs, width)
    return (wide + scale * attended).astype(jnp.bfloat16)


def per_device(tokens, kv_pool, page_table, lengths, migrate_ids, norm_gain, out_scale):
    inputs = tokens[0]
    pool = kv_pool[0, 0]
    table = page_table[0]
    lens = lengths[0]
    moving = migrate_ids[0]
    gain = norm_gain[0]
    scale = out_scale[0]
    steps, reqs, width = inputs.shape
    page_len = pool.shape[3]
    chosen = table[moving]
    outgoing = pool[chosen]
    spots = jnp.arange(chosen.shape[1])[:, None] * page_len + jnp.arange(page_len)[None, :]
    keep = spots[None, :, :] < lens[moving][:, None, None]
    outgoing = jnp.where(keep[:, :, None, None, :, None], outgoing, jnp.zeros((), jnp.bfloat16))
    received = partner(outgoing, "inst", 0)
    keys = jnp.swapaxes(pool[:, 0][table], -1, -2)
    values = pool[:, 1][table]
    lens_used = lens
    section = lax.axis_index("section")
    count = lax.axis_size("section")
    chunks = CHUNKS
    block = reqs // chunks

    def tick(k, carry):
        incoming, finished = carry
        item = k - section
        live = jnp.logical_and(item >= 0, item < chunks)
        start = jnp.clip(item, 0, chunks - 1) * block
        zero = jnp.zeros((), jnp.int32)
        first = lax.dynamic_slice_in_dim(inputs, start, block, 1)
        rows = jnp.where(section == 0, first, incoming)
        part_keys = lax.dynamic_slice_in_dim(keys, start, block, 0)
        part_values = lax.dynamic_slice_in_dim(values, start, block, 0)
        part_lens = lax.dynamic_slice_in_dim(lens_used, start, block, 0)
        result = layer(rows, part_keys, part_values, part_lens, gain, scale)
        previous = lax.dynamic_slice_in_dim(finished, start, block, 1)
        finished = lax.dynamic_update_slice(
            finished, jnp.where(live, result, previous), (zero, start, zero)
        )
        passed = passed_along(result, "section", 1)
        return (passed, finished)

    start_carry = (
        jnp.zeros((steps, block, width), jnp.bfloat16),
        jnp.zeros((steps, reqs, width), jnp.bfloat16),
    )
    _, finished = lax.fori_loop(0, chunks + count - 1, tick, start_carry)
    handed = partner(finished[:, moving], "inst", 0)
    finished = finished.at[:, moving].set(handed)
    return (finished[None, None], received[None, None])


def solution(mesh):
    in_specs = (
        P(("groups", "inst"), None, None, None),
        P(("groups", "inst"), "section", None, None, None, None, None),
        P(("groups", "inst"), None, None),
        P(("groups", "inst"), None),
        P(("groups", "inst"), None),
        P("section", None),
        P("section", None),
    )
    out_specs = (
        P(("groups", "inst"), "section", None, None, None),
        P(("groups", "inst"), "section", None, None, None, None, None, None),
    )
    return jax.shard_map(
        per_device, mesh=mesh, in_specs=in_specs, out_specs=out_specs, check_vma=False
    )
```

```python
import math

import jax
import jax.numpy as jnp
from jax import lax
from jax.sharding import PartitionSpec as P

CHUNKS = 2


def partner(block, axis, stride):
    count = lax.axis_size(axis)
    route = []
    for low in range(count):
        high = low | 1 << stride
        if high != low and high < count:
            route += [(low, high), (high, low)]
    return lax.ppermute(block, axis, route)


def passed_along(array, axis, by):
    peers = lax.axis_size(axis)
    pairs = [(i, i + by) for i in range(peers) if 0 <= i + by < peers]
    return lax.ppermute(array, axis, pairs)


def layer(rows, keys, values, lens, gain, scale):
    steps, reqs, width = rows.shape
    pages = keys.shape[1]
    kv_heads = keys.shape[2]
    page_len = keys.shape[3]
    head = keys.shape[4]
    group = width // (kv_heads * head)
    wide = rows.astype(jnp.float32)
    normed = wide * lax.rsqrt(jnp.mean(wide * wide, axis=-1, keepdims=True) + 1e-05) * gain
    heads = normed.reshape(steps, reqs, kv_heads, group, head)
    query = jnp.transpose(heads.astype(jnp.bfloat16), (1, 2, 0, 3, 4))
    query = query.reshape(reqs, kv_heads, steps * group, head)
    fresh = jnp.mean(heads, axis=3).astype(jnp.bfloat16)
    fresh = jnp.transpose(fresh, (1, 2, 0, 3))
    factor = 1.0 / math.sqrt(head)
    wide_query = jnp.broadcast_to(query[:, None], (reqs, pages) + query.shape[1:])
    cache_scores = (
        jnp.einsum("rjgxd,rjgpd->rjgxp", wide_query, keys, preferred_element_type=jnp.float32)
        * factor
    )
    positions = jnp.arange(pages)[:, None] * page_len + jnp.arange(page_len)[None, :]
    live = positions[None] < lens[:, None, None]
    cache_scores = jnp.where(live[:, :, None, None, :], cache_scores, -1e30)
    new_scores = (
        jnp.einsum("rgxd,rgsd->rgxs", query, fresh, preferred_element_type=jnp.float32) * factor
    )
    step_of = jnp.arange(steps * group) // group
    done = jnp.arange(steps)[None, :] <= step_of[:, None]
    new_scores = jnp.where(done[None, None], new_scores, -1e30)
    top = jnp.maximum(
        jnp.max(cache_scores, axis=(1, 4)), jnp.max(new_scores, axis=-1)
    )[..., None]
    cache_exp = jnp.exp(cache_scores - top[:, None])
    new_exp = jnp.exp(new_scores - top)
    total = jnp.sum(cache_exp, axis=(1, 4))[..., None] + jnp.sum(new_exp, axis=-1, keepdims=True)
    cache_w = (cache_exp / total[:, None]).astype(jnp.bfloat16)
    new_w = (new_exp / total).astype(jnp.bfloat16)
    attended = jnp.einsum(
        "rjgxp,rjgpd->rjgxd", cache_w, values, preferred_element_type=jnp.float32
    ).sum(axis=1)
    attended = attended + jnp.einsum(
        "rgxs,rgsd->rgxd", new_w, fresh, preferred_element_type=jnp.float32
    )
    attended = attended.reshape(reqs, kv_heads, steps, group, head)
    attended = jnp.transpose(attended, (2, 0, 1, 3, 4)).reshape(steps, reqs, width)
    return (wide + scale * attended).astype(jnp.bfloat16)


def per_device(tokens, kv_pool, page_table, lengths, migrate_ids, norm_gain, out_scale):
    inputs = tokens[0]
    pool = kv_pool[0, 0]
    table = page_table[0]
    lens = lengths[0]
    moving = migrate_ids[0]
    gain = norm_gain[0]
    scale = out_scale[0]
    steps, reqs, width = inputs.shape
    page_len = pool.shape[3]
    chosen = table[moving]
    outgoing = pool[chosen]
    spots = jnp.arange(chosen.shape[1])[:, None] * page_len + jnp.arange(page_len)[None, :]
    keep = spots[None, :, :] < lens[moving][:, None, None]
    outgoing = jnp.where(keep[:, :, None, None, :, None], outgoing, jnp.zeros((), jnp.bfloat16))
    received = partner(outgoing, "inst", 0)
    keys = pool[:, 0][table]
    values = pool[:, 1][table]
    lens_used = lens
    section = lax.axis_index("section")
    count = lax.axis_size("section")
    chunks = CHUNKS
    block = reqs // chunks

    incoming = jnp.zeros((steps, block, width), jnp.bfloat16)
    finished = jnp.zeros((steps, reqs, width), jnp.bfloat16)
    zero = jnp.zeros((), jnp.int32)
    for k in range(chunks + count - 1):
        item = k - section
        live = jnp.logical_and(item >= 0, item < chunks)
        start = jnp.clip(item, 0, chunks - 1) * block
        first = lax.dynamic_slice_in_dim(inputs, start, block, 1)
        rows = jnp.where(section == 0, first, incoming)
        part_keys = lax.dynamic_slice_in_dim(keys, start, block, 0)
        part_values = lax.dynamic_slice_in_dim(values, start, block, 0)
        part_lens = lax.dynamic_slice_in_dim(lens_used, start, block, 0)
        result = layer(rows, part_keys, part_values, part_lens, gain, scale)
        previous = lax.dynamic_slice_in_dim(finished, start, block, 1)
        finished = lax.dynamic_update_slice(
            finished, jnp.where(live, result, previous), (zero, start, zero)
        )
        pairs = [(s, s + 1) for s in range(count - 1) if 0 <= k - s < chunks]
        if pairs:
            incoming = lax.ppermute(result, "section", pairs)
    handed = partner(finished[:, moving], "inst", 0)
    finished = finished.at[:, moving].set(handed)
    return (finished[None, None], received[None, None])


def solution(mesh):
    in_specs = (
        P(("groups", "inst"), None, None, None),
        P(("groups", "inst"), "section", None, None, None, None, None),
        P(("groups", "inst"), None, None),
        P(("groups", "inst"), None),
        P(("groups", "inst"), None),
        P("section", None),
        P("section", None),
    )
    out_specs = (
        P(("groups", "inst"), "section", None, None, None),
        P(("groups", "inst"), "section", None, None, None, None, None, None),
    )
    return jax.shard_map(
        per_device, mesh=mesh, in_specs=in_specs, out_specs=out_specs, check_vma=False
    )
```

```python
import math

import jax
import jax.numpy as jnp
from jax import lax
from jax.sharding import PartitionSpec as P

CHUNKS = 2


def partner(block, axis, stride):
    count = lax.axis_size(axis)
    route = []
    for low in range(count):
        high = low | 1 << stride
        if high != low and high < count:
            route += [(low, high), (high, low)]
    return lax.ppermute(block, axis, route)


def passed_along(array, axis, by):
    peers = lax.axis_size(axis)
    pairs = [(i, i + by) for i in range(peers) if 0 <= i + by < peers]
    return lax.ppermute(array, axis, pairs)


def layer(rows, keys, values, lens, gain, scale):
    steps, reqs, width = rows.shape
    pages = keys.shape[1]
    kv_heads = keys.shape[2]
    page_len = keys.shape[3]
    head = keys.shape[4]
    group = width // (kv_heads * head)
    wide = rows.astype(jnp.float32)
    normed = wide * lax.rsqrt(jnp.mean(wide * wide, axis=-1, keepdims=True) + 1e-05) * gain
    heads = normed.reshape(steps, reqs, kv_heads, group, head)
    query = jnp.transpose(heads.astype(jnp.bfloat16), (1, 2, 0, 3, 4))
    query = query.reshape(reqs, kv_heads, steps * group, head)
    fresh = jnp.mean(heads, axis=3).astype(jnp.bfloat16)
    fresh = jnp.transpose(fresh, (1, 2, 0, 3))
    factor = 1.0 / math.sqrt(head)
    wide_query = jnp.broadcast_to(query[:, None], (reqs, pages) + query.shape[1:])
    cache_scores = (
        jnp.einsum("rjgxd,rjgpd->rjgxp", wide_query, keys, preferred_element_type=jnp.float32)
        * factor
    )
    positions = jnp.arange(pages)[:, None] * page_len + jnp.arange(page_len)[None, :]
    live = positions[None] < lens[:, None, None]
    cache_scores = jnp.where(live[:, :, None, None, :], cache_scores, -1e30)
    new_scores = (
        jnp.einsum("rgxd,rgsd->rgxs", query, fresh, preferred_element_type=jnp.float32) * factor
    )
    step_of = jnp.arange(steps * group) // group
    done = jnp.arange(steps)[None, :] <= step_of[:, None]
    new_scores = jnp.where(done[None, None], new_scores, -1e30)
    top = jnp.maximum(
        jnp.max(cache_scores, axis=(1, 4)), jnp.max(new_scores, axis=-1)
    )[..., None]
    cache_exp = jnp.exp(cache_scores - top[:, None])
    new_exp = jnp.exp(new_scores - top)
    total = jnp.sum(cache_exp, axis=(1, 4))[..., None] + jnp.sum(new_exp, axis=-1, keepdims=True)
    cache_w = (cache_exp / total[:, None]).astype(jnp.bfloat16)
    new_w = (new_exp / total).astype(jnp.bfloat16)
    attended = jnp.einsum(
        "rjgxp,rjgpd->rjgxd", cache_w, values, preferred_element_type=jnp.float32
    ).sum(axis=1)
    attended = attended + jnp.einsum(
        "rgxs,rgsd->rgxd", new_w, fresh, preferred_element_type=jnp.float32
    )
    attended = attended.reshape(reqs, kv_heads, steps, group, head)
    attended = jnp.transpose(attended, (2, 0, 1, 3, 4)).reshape(steps, reqs, width)
    return (wide + scale * attended).astype(jnp.bfloat16)


def per_device(tokens, kv_pool, page_table, lengths, migrate_ids, norm_gain, out_scale):
    inputs = tokens[0]
    pool = kv_pool[0, 0]
    table = page_table[0]
    lens = lengths[0]
    moving = migrate_ids[0]
    gain = norm_gain[0]
    scale = out_scale[0]
    steps, reqs, width = inputs.shape
    page_len = pool.shape[3]
    chosen = table[moving]
    outgoing = pool[chosen]
    spots = jnp.arange(chosen.shape[1])[:, None] * page_len + jnp.arange(page_len)[None, :]
    keep = spots[None, :, :] < lens[moving][:, None, None]
    outgoing = jnp.where(keep[:, :, None, None, :, None], outgoing, jnp.zeros((), jnp.bfloat16))
    received = partner(outgoing, "inst", 0)
    flat_pool = pool.reshape((-1,) + pool.shape[2:])
    keys = flat_pool[table * 2]
    values = flat_pool[table * 2 + 1]
    lens_used = lens
    section = lax.axis_index("section")
    count = lax.axis_size("section")
    chunks = CHUNKS
    block = reqs // chunks

    incoming = jnp.zeros((steps, block, width), jnp.bfloat16)
    finished = jnp.zeros((steps, reqs, width), jnp.bfloat16)
    zero = jnp.zeros((), jnp.int32)
    for k in range(chunks + count - 1):
        item = k - section
        live = jnp.logical_and(item >= 0, item < chunks)
        start = jnp.clip(item, 0, chunks - 1) * block
        if k > 0:
            start, incoming = lax.optimization_barrier((start, incoming))
        first = lax.dynamic_slice_in_dim(inputs, start, block, 1)
        rows = jnp.where(section == 0, first, incoming)
        part_keys = lax.dynamic_slice_in_dim(keys, start, block, 0)
        part_values = lax.dynamic_slice_in_dim(values, start, block, 0)
        part_lens = lax.dynamic_slice_in_dim(lens_used, start, block, 0)
        result = layer(rows, part_keys, part_values, part_lens, gain, scale)
        previous = lax.dynamic_slice_in_dim(finished, start, block, 1)
        finished = lax.dynamic_update_slice(
            finished, jnp.where(live, result, previous), (zero, start, zero)
        )
        pairs = [(s, s + 1) for s in range(count - 1) if 0 <= k - s < chunks]
        if pairs:
            incoming = lax.ppermute(result, "section", pairs)
    handed = partner(finished[:, moving], "inst", 0)
    finished = finished.at[:, moving].set(handed)
    return (finished[None, None], received[None, None])


def solution(mesh):
    in_specs = (
        P(("groups", "inst"), None, None, None),
        P(("groups", "inst"), "section", None, None, None, None, None),
        P(("groups", "inst"), None, None),
        P(("groups", "inst"), None),
        P(("groups", "inst"), None),
        P("section", None),
        P("section", None),
    )
    out_specs = (
        P(("groups", "inst"), "section", None, None, None),
        P(("groups", "inst"), "section", None, None, None, None, None, None),
    )
    return jax.shard_map(
        per_device, mesh=mesh, in_specs=in_specs, out_specs=out_specs, check_vma=False
    )
```

```python
import math

import jax
import jax.numpy as jnp
from jax import lax
from jax.sharding import PartitionSpec as P

CHUNKS = 4


def partner(block, axis, stride):
    count = lax.axis_size(axis)
    route = []
    for low in range(count):
        high = low | 1 << stride
        if high != low and high < count:
            route += [(low, high), (high, low)]
    return lax.ppermute(block, axis, route)


def passed_along(array, axis, by):
    peers = lax.axis_size(axis)
    pairs = [(i, i + by) for i in range(peers) if 0 <= i + by < peers]
    return lax.ppermute(array, axis, pairs)


def layer(rows, keys, values, lens, gain, scale):
    steps, reqs, width = rows.shape
    pages = keys.shape[1]
    kv_heads = keys.shape[2]
    page_len = keys.shape[3]
    head = keys.shape[4]
    group = width // (kv_heads * head)
    wide = rows.astype(jnp.float32)
    normed = wide * lax.rsqrt(jnp.mean(wide * wide, axis=-1, keepdims=True) + 1e-05) * gain
    heads = normed.reshape(steps, reqs, kv_heads, group, head)
    query = jnp.transpose(heads.astype(jnp.bfloat16), (1, 2, 0, 3, 4))
    query = query.reshape(reqs, kv_heads, steps * group, head)
    fresh = jnp.mean(heads, axis=3).astype(jnp.bfloat16)
    fresh = jnp.transpose(fresh, (1, 2, 0, 3))
    factor = 1.0 / math.sqrt(head)
    wide_query = jnp.broadcast_to(query[:, None], (reqs, pages) + query.shape[1:])
    cache_scores = (
        jnp.einsum("rjgxd,rjgpd->rjgxp", wide_query, keys, preferred_element_type=jnp.float32)
        * factor
    )
    positions = jnp.arange(pages)[:, None] * page_len + jnp.arange(page_len)[None, :]
    live = positions[None] < lens[:, None, None]
    cache_scores = jnp.where(live[:, :, None, None, :], cache_scores, -1e30)
    new_scores = (
        jnp.einsum("rgxd,rgsd->rgxs", query, fresh, preferred_element_type=jnp.float32) * factor
    )
    step_of = jnp.arange(steps * group) // group
    done = jnp.arange(steps)[None, :] <= step_of[:, None]
    new_scores = jnp.where(done[None, None], new_scores, -1e30)
    top = jnp.maximum(
        jnp.max(cache_scores, axis=(1, 4)), jnp.max(new_scores, axis=-1)
    )[..., None]
    cache_exp = jnp.exp(cache_scores - top[:, None])
    new_exp = jnp.exp(new_scores - top)
    total = jnp.sum(cache_exp, axis=(1, 4))[..., None] + jnp.sum(new_exp, axis=-1, keepdims=True)
    cache_w = (cache_exp / total[:, None]).astype(jnp.bfloat16)
    new_w = (new_exp / total).astype(jnp.bfloat16)
    attended = jnp.einsum(
        "rjgxp,rjgpd->rjgxd", cache_w, values, preferred_element_type=jnp.float32
    ).sum(axis=1)
    attended = attended + jnp.einsum(
        "rgxs,rgsd->rgxd", new_w, fresh, preferred_element_type=jnp.float32
    )
    attended = attended.reshape(reqs, kv_heads, steps, group, head)
    attended = jnp.transpose(attended, (2, 0, 1, 3, 4)).reshape(steps, reqs, width)
    return (wide + scale * attended).astype(jnp.bfloat16)


def per_device(tokens, kv_pool, page_table, lengths, migrate_ids, norm_gain, out_scale):
    inputs = tokens[0]
    pool = kv_pool[0, 0]
    table = page_table[0]
    lens = lengths[0]
    moving = migrate_ids[0]
    gain = norm_gain[0]
    scale = out_scale[0]
    steps, reqs, width = inputs.shape
    page_len = pool.shape[3]
    chosen = table[moving]
    outgoing = pool[chosen]
    spots = jnp.arange(chosen.shape[1])[:, None] * page_len + jnp.arange(page_len)[None, :]
    keep = spots[None, :, :] < lens[moving][:, None, None]
    outgoing = jnp.where(keep[:, :, None, None, :, None], outgoing, jnp.zeros((), jnp.bfloat16))
    received = partner(outgoing, "inst", 0)
    flat_pool = pool.reshape((-1,) + pool.shape[2:])
    keys = flat_pool[table * 2]
    values = flat_pool[table * 2 + 1]
    lens_used = lens
    section = lax.axis_index("section")
    count = lax.axis_size("section")
    chunks = CHUNKS
    block = reqs // chunks

    incoming = jnp.zeros((steps, block, width), jnp.bfloat16)
    finished = jnp.zeros((steps, reqs, width), jnp.bfloat16)
    zero = jnp.zeros((), jnp.int32)
    for k in range(chunks + count - 1):
        item = k - section
        live = jnp.logical_and(item >= 0, item < chunks)
        start = jnp.clip(item, 0, chunks - 1) * block
        if k > 0:
            start, incoming = lax.optimization_barrier((start, incoming))
        first = lax.dynamic_slice_in_dim(inputs, start, block, 1)
        rows = jnp.where(section == 0, first, incoming)
        part_keys = lax.dynamic_slice_in_dim(keys, start, block, 0)
        part_values = lax.dynamic_slice_in_dim(values, start, block, 0)
        part_lens = lax.dynamic_slice_in_dim(lens_used, start, block, 0)
        result = layer(rows, part_keys, part_values, part_lens, gain, scale)
        previous = lax.dynamic_slice_in_dim(finished, start, block, 1)
        finished = lax.dynamic_update_slice(
            finished, jnp.where(live, result, previous), (zero, start, zero)
        )
        pairs = [(s, s + 1) for s in range(count - 1) if 0 <= k - s < chunks]
        if pairs:
            incoming = lax.ppermute(result, "section", pairs)
    handed = partner(finished[:, moving], "inst", 0)
    finished = finished.at[:, moving].set(handed)
    return (finished[None, None], received[None, None])


def solution(mesh):
    in_specs = (
        P(("groups", "inst"), None, None, None),
        P(("groups", "inst"), "section", None, None, None, None, None),
        P(("groups", "inst"), None, None),
        P(("groups", "inst"), None),
        P(("groups", "inst"), None),
        P("section", None),
        P("section", None),
    )
    out_specs = (
        P(("groups", "inst"), "section", None, None, None),
        P(("groups", "inst"), "section", None, None, None, None, None, None),
    )
    return jax.shard_map(
        per_device, mesh=mesh, in_specs=in_specs, out_specs=out_specs, check_vma=False
    )
```

```python
import math

import jax
import jax.numpy as jnp
from jax import lax
from jax.sharding import PartitionSpec as P
from jax.experimental import pallas as pl
from jax.experimental.pallas import tpu as pltpu

CHUNKS = 4


def partner(block, axis, stride):
    count = lax.axis_size(axis)
    route = []
    for low in range(count):
        high = low | 1 << stride
        if high != low and high < count:
            route += [(low, high), (high, low)]
    return lax.ppermute(block, axis, route)


def passed_along(array, axis, by):
    peers = lax.axis_size(axis)
    pairs = [(i, i + by) for i in range(peers) if 0 <= i + by < peers]
    return lax.ppermute(array, axis, pairs)


def layer(rows, keys, values, lens, gain, scale):
    steps, reqs, width = rows.shape
    pages = keys.shape[1]
    kv_heads = keys.shape[2]
    page_len = keys.shape[3]
    head = keys.shape[4]
    group = width // (kv_heads * head)
    wide = rows.astype(jnp.float32)
    normed = wide * lax.rsqrt(jnp.mean(wide * wide, axis=-1, keepdims=True) + 1e-05) * gain
    heads = normed.reshape(steps, reqs, kv_heads, group, head)
    query = jnp.transpose(heads.astype(jnp.bfloat16), (1, 2, 0, 3, 4))
    query = query.reshape(reqs, kv_heads, steps * group, head)
    fresh = jnp.mean(heads, axis=3).astype(jnp.bfloat16)
    fresh = jnp.transpose(fresh, (1, 2, 0, 3))
    factor = 1.0 / math.sqrt(head)
    wide_query = jnp.broadcast_to(query[:, None], (reqs, pages) + query.shape[1:])
    cache_scores = (
        jnp.einsum("rjgxd,rjgpd->rjgxp", wide_query, keys, preferred_element_type=jnp.float32)
        * factor
    )
    positions = jnp.arange(pages)[:, None] * page_len + jnp.arange(page_len)[None, :]
    live = positions[None] < lens[:, None, None]
    cache_scores = jnp.where(live[:, :, None, None, :], cache_scores, -1e30)
    new_scores = (
        jnp.einsum("rgxd,rgsd->rgxs", query, fresh, preferred_element_type=jnp.float32) * factor
    )
    step_of = jnp.arange(steps * group) // group
    done = jnp.arange(steps)[None, :] <= step_of[:, None]
    new_scores = jnp.where(done[None, None], new_scores, -1e30)
    top = jnp.maximum(
        jnp.max(cache_scores, axis=(1, 4)), jnp.max(new_scores, axis=-1)
    )[..., None]
    cache_exp = jnp.exp(cache_scores - top[:, None])
    new_exp = jnp.exp(new_scores - top)
    total = jnp.sum(cache_exp, axis=(1, 4))[..., None] + jnp.sum(new_exp, axis=-1, keepdims=True)
    cache_w = (cache_exp / total[:, None]).astype(jnp.bfloat16)
    new_w = (new_exp / total).astype(jnp.bfloat16)
    attended = jnp.einsum(
        "rjgxp,rjgpd->rjgxd", cache_w, values, preferred_element_type=jnp.float32
    ).sum(axis=1)
    attended = attended + jnp.einsum(
        "rgxs,rgsd->rgxd", new_w, fresh, preferred_element_type=jnp.float32
    )
    attended = attended.reshape(reqs, kv_heads, steps, group, head)
    attended = jnp.transpose(attended, (2, 0, 1, 3, 4)).reshape(steps, reqs, width)
    return (wide + scale * attended).astype(jnp.bfloat16)


def gather_kernel(table_ref, moving_ref, pool_ref, keys_ref, values_ref, out_ref, sems):
    reqs, pages = keys_ref.shape[0], keys_ref.shape[1]
    copies = []
    for r in range(reqs):
        for j in range(pages):
            page = table_ref[r * pages + j]
            copies.append(
                pltpu.make_async_copy(pool_ref.at[page, 0], keys_ref.at[r, j], sems.at[len(copies)])
            )
            copies.append(
                pltpu.make_async_copy(pool_ref.at[page, 1], values_ref.at[r, j], sems.at[len(copies)])
            )
    for m in range(out_ref.shape[0]):
        for j in range(pages):
            page = table_ref[moving_ref[m] * pages + j]
            copies.append(
                pltpu.make_async_copy(pool_ref.at[page], out_ref.at[m, j], sems.at[len(copies)])
            )
    for copy in copies:
        copy.start()
    for copy in copies:
        copy.wait()


def gather_pages(pool, table, moving):
    reqs, pages = table.shape
    kv_heads, page_len, head = pool.shape[2:]
    count = 2 * reqs * pages + moving.shape[0] * pages
    any_spec = pl.BlockSpec(memory_space=pl.ANY)
    grid_spec = pltpu.PrefetchScalarGridSpec(
        num_scalar_prefetch=2,
        grid=(1,),
        in_specs=[any_spec],
        out_specs=[any_spec, any_spec, any_spec],
        scratch_shapes=[pltpu.SemaphoreType.DMA((count,))],
    )
    half = jax.ShapeDtypeStruct((reqs, pages, kv_heads, page_len, head), pool.dtype)
    whole = jax.ShapeDtypeStruct((moving.shape[0], pages) + pool.shape[1:], pool.dtype)
    return pl.pallas_call(
        gather_kernel, grid_spec=grid_spec, out_shape=[half, half, whole]
    )(table.reshape(-1), moving, pool)


def per_device(tokens, kv_pool, page_table, lengths, migrate_ids, norm_gain, out_scale):
    inputs = tokens[0]
    pool = kv_pool[0, 0]
    table = page_table[0]
    lens = lengths[0]
    moving = migrate_ids[0]
    gain = norm_gain[0]
    scale = out_scale[0]
    steps, reqs, width = inputs.shape
    page_len = pool.shape[3]
    keys, values, outgoing = gather_pages(pool, table, moving)
    received = partner(outgoing, "inst", 0)
    arrived_lens = partner(lens[moving], "inst", 0)
    spots = jnp.arange(table.shape[1])[:, None] * page_len + jnp.arange(page_len)[None, :]
    keep = spots[None, :, :] < arrived_lens[:, None, None]
    arrived = jnp.where(keep[:, :, None, None, :, None], received, jnp.zeros((), jnp.bfloat16))
    lens_used = lens
    section = lax.axis_index("section")
    count = lax.axis_size("section")
    chunks = CHUNKS
    block = reqs // chunks

    incoming = jnp.zeros((steps, block, width), jnp.bfloat16)
    finished = jnp.zeros((steps, reqs, width), jnp.bfloat16)
    zero = jnp.zeros((), jnp.int32)
    for k in range(chunks + count - 1):
        item = k - section
        live = jnp.logical_and(item >= 0, item < chunks)
        start = jnp.clip(item, 0, chunks - 1) * block
        if k > 0:
            start, incoming = lax.optimization_barrier((start, incoming))
        first = lax.dynamic_slice_in_dim(inputs, start, block, 1)
        rows = jnp.where(section == 0, first, incoming)
        part_keys = lax.dynamic_slice_in_dim(keys, start, block, 0)
        part_values = lax.dynamic_slice_in_dim(values, start, block, 0)
        part_lens = lax.dynamic_slice_in_dim(lens_used, start, block, 0)
        result = layer(rows, part_keys, part_values, part_lens, gain, scale)
        previous = lax.dynamic_slice_in_dim(finished, start, block, 1)
        finished = lax.dynamic_update_slice(
            finished, jnp.where(live, result, previous), (zero, start, zero)
        )
        pairs = [(s, s + 1) for s in range(count - 1) if 0 <= k - s < chunks]
        if pairs:
            incoming = lax.ppermute(result, "section", pairs)
    handed = partner(finished[:, moving], "inst", 0)
    finished = finished.at[:, moving].set(handed)
    return (finished[None, None], arrived[None, None])


def solution(mesh):
    in_specs = (
        P(("groups", "inst"), None, None, None),
        P(("groups", "inst"), "section", None, None, None, None, None),
        P(("groups", "inst"), None, None),
        P(("groups", "inst"), None),
        P(("groups", "inst"), None),
        P("section", None),
        P("section", None),
    )
    out_specs = (
        P(("groups", "inst"), "section", None, None, None),
        P(("groups", "inst"), "section", None, None, None, None, None, None),
    )
    return jax.shard_map(
        per_device, mesh=mesh, in_specs=in_specs, out_specs=out_specs, check_vma=False
    )
```

```python
import math

import jax
import jax.numpy as jnp
from jax import lax
from jax.sharding import PartitionSpec as P

CHUNKS = 4


def partner(block, axis, stride):
    count = lax.axis_size(axis)
    route = []
    for low in range(count):
        high = low | 1 << stride
        if high != low and high < count:
            route += [(low, high), (high, low)]
    return lax.ppermute(block, axis, route)


def passed_along(array, axis, by):
    peers = lax.axis_size(axis)
    pairs = [(i, i + by) for i in range(peers) if 0 <= i + by < peers]
    return lax.ppermute(array, axis, pairs)


def layer(rows, keys, values, lens, gain, scale):
    steps, reqs, width = rows.shape
    pages = keys.shape[1]
    kv_heads = keys.shape[2]
    page_len = keys.shape[3]
    head = keys.shape[4]
    group = width // (kv_heads * head)
    wide = rows.astype(jnp.float32)
    normed = wide * lax.rsqrt(jnp.mean(wide * wide, axis=-1, keepdims=True) + 1e-05) * gain
    heads = normed.reshape(steps, reqs, kv_heads, group, head)
    query = jnp.transpose(heads.astype(jnp.bfloat16), (1, 2, 0, 3, 4))
    query = query.reshape(reqs, kv_heads, steps * group, head)
    fresh = jnp.mean(heads, axis=3).astype(jnp.bfloat16)
    fresh = jnp.transpose(fresh, (1, 2, 0, 3))
    factor = 1.0 / math.sqrt(head)
    wide_query = jnp.broadcast_to(query[:, None], (reqs, pages) + query.shape[1:])
    cache_scores = (
        jnp.einsum("rjgxd,rjgpd->rjgxp", wide_query, keys, preferred_element_type=jnp.float32)
        * factor
    )
    positions = jnp.arange(pages)[:, None] * page_len + jnp.arange(page_len)[None, :]
    live = positions[None] < lens[:, None, None]
    cache_scores = jnp.where(live[:, :, None, None, :], cache_scores, -1e30)
    new_scores = (
        jnp.einsum("rgxd,rgsd->rgxs", query, fresh, preferred_element_type=jnp.float32) * factor
    )
    step_of = jnp.arange(steps * group) // group
    done = jnp.arange(steps)[None, :] <= step_of[:, None]
    new_scores = jnp.where(done[None, None], new_scores, -1e30)
    top = jnp.maximum(
        jnp.max(cache_scores, axis=(1, 4)), jnp.max(new_scores, axis=-1)
    )[..., None]
    cache_exp = jnp.exp(cache_scores - top[:, None])
    new_exp = jnp.exp(new_scores - top)
    total = jnp.sum(cache_exp, axis=(1, 4))[..., None] + jnp.sum(new_exp, axis=-1, keepdims=True)
    cache_w = (cache_exp / total[:, None]).astype(jnp.bfloat16)
    new_w = (new_exp / total).astype(jnp.bfloat16)
    attended = jnp.einsum(
        "rjgxp,rjgpd->rjgxd", cache_w, values, preferred_element_type=jnp.float32
    ).sum(axis=1)
    attended = attended + jnp.einsum(
        "rgxs,rgsd->rgxd", new_w, fresh, preferred_element_type=jnp.float32
    )
    attended = attended.reshape(reqs, kv_heads, steps, group, head)
    attended = jnp.transpose(attended, (2, 0, 1, 3, 4)).reshape(steps, reqs, width)
    return (wide + scale * attended).astype(jnp.bfloat16)


def per_device(tokens, kv_pool, page_table, lengths, migrate_ids, norm_gain, out_scale):
    inputs = tokens[0]
    pool = kv_pool[0, 0]
    table = page_table[0]
    lens = lengths[0]
    moving = migrate_ids[0]
    gain = norm_gain[0]
    scale = out_scale[0]
    steps, reqs, width = inputs.shape
    page_len = pool.shape[3]
    chosen = table[moving]
    outgoing = jnp.stack(
        [
            jnp.stack([lax.dynamic_index_in_dim(pool, chosen[m, j], 0, False) for j in range(chosen.shape[1])])
            for m in range(chosen.shape[0])
        ]
    )
    received = partner(outgoing, "inst", 0)
    arrived_lens = partner(lens[moving], "inst", 0)
    spots = jnp.arange(chosen.shape[1])[:, None] * page_len + jnp.arange(page_len)[None, :]
    keep = spots[None, :, :] < arrived_lens[:, None, None]
    arrived = jnp.where(keep[:, :, None, None, :, None], received, jnp.zeros((), jnp.bfloat16))
    flat_pool = pool.reshape((-1,) + pool.shape[2:])
    keys = flat_pool[table * 2]
    values = flat_pool[table * 2 + 1]
    lens_used = lens
    section = lax.axis_index("section")
    count = lax.axis_size("section")
    chunks = CHUNKS
    block = reqs // chunks

    incoming = jnp.zeros((steps, block, width), jnp.bfloat16)
    finished = jnp.zeros((steps, reqs, width), jnp.bfloat16)
    zero = jnp.zeros((), jnp.int32)
    for k in range(chunks + count - 1):
        item = k - section
        live = jnp.logical_and(item >= 0, item < chunks)
        start = jnp.clip(item, 0, chunks - 1) * block
        if k > 0:
            start, incoming = lax.optimization_barrier((start, incoming))
        first = lax.dynamic_slice_in_dim(inputs, start, block, 1)
        rows = jnp.where(section == 0, first, incoming)
        part_keys = lax.dynamic_slice_in_dim(keys, start, block, 0)
        part_values = lax.dynamic_slice_in_dim(values, start, block, 0)
        part_lens = lax.dynamic_slice_in_dim(lens_used, start, block, 0)
        result = layer(rows, part_keys, part_values, part_lens, gain, scale)
        previous = lax.dynamic_slice_in_dim(finished, start, block, 1)
        finished = lax.dynamic_update_slice(
            finished, jnp.where(live, result, previous), (zero, start, zero)
        )
        pairs = [(s, s + 1) for s in range(count - 1) if 0 <= k - s < chunks]
        if pairs:
            incoming = lax.ppermute(result, "section", pairs)
    handed = partner(finished[:, moving], "inst", 0)
    finished = finished.at[:, moving].set(handed)
    return (finished[None, None], arrived[None, None])


def solution(mesh):
    in_specs = (
        P(("groups", "inst"), None, None, None),
        P(("groups", "inst"), "section", None, None, None, None, None),
        P(("groups", "inst"), None, None),
        P(("groups", "inst"), None),
        P(("groups", "inst"), None),
        P("section", None),
        P("section", None),
    )
    out_specs = (
        P(("groups", "inst"), "section", None, None, None),
        P(("groups", "inst"), "section", None, None, None, None, None, None),
    )
    return jax.shard_map(
        per_device, mesh=mesh, in_specs=in_specs, out_specs=out_specs, check_vma=False
    )
```

```python
import math

import jax
import jax.numpy as jnp
from jax import lax
from jax.sharding import PartitionSpec as P

CHUNKS = 4


def partner(block, axis, stride):
    count = lax.axis_size(axis)
    route = []
    for low in range(count):
        high = low | 1 << stride
        if high != low and high < count:
            route += [(low, high), (high, low)]
    return lax.ppermute(block, axis, route)


def passed_along(array, axis, by):
    peers = lax.axis_size(axis)
    pairs = [(i, i + by) for i in range(peers) if 0 <= i + by < peers]
    return lax.ppermute(array, axis, pairs)


def layer(rows, keys, values, lens, gain, scale):
    steps, reqs, width = rows.shape
    pages = keys.shape[1]
    kv_heads = keys.shape[2]
    page_len = keys.shape[3]
    head = keys.shape[4]
    group = width // (kv_heads * head)
    wide = rows.astype(jnp.float32)
    normed = wide * lax.rsqrt(jnp.mean(wide * wide, axis=-1, keepdims=True) + 1e-05) * gain
    heads = normed.reshape(steps, reqs, kv_heads, group, head)
    query = jnp.transpose(heads.astype(jnp.bfloat16), (1, 2, 0, 3, 4))
    query = query.reshape(reqs, kv_heads, steps * group, head)
    fresh = jnp.mean(heads, axis=3).astype(jnp.bfloat16)
    fresh = jnp.transpose(fresh, (1, 2, 0, 3))
    factor = 1.0 / math.sqrt(head)
    wide_query = jnp.broadcast_to(query[:, None], (reqs, pages) + query.shape[1:])
    cache_scores = (
        jnp.einsum("rjgpd,rjgxd->rjgpx", keys, wide_query, preferred_element_type=jnp.float32)
        * factor
    )
    positions = jnp.arange(pages)[:, None] * page_len + jnp.arange(page_len)[None, :]
    live = positions[None] < lens[:, None, None]
    cache_scores = jnp.where(live[:, :, None, :, None], cache_scores, -1e30)
    new_scores = (
        jnp.einsum("rgxd,rgsd->rgxs", query, fresh, preferred_element_type=jnp.float32) * factor
    )
    step_of = jnp.arange(steps * group) // group
    done = jnp.arange(steps)[None, :] <= step_of[:, None]
    new_scores = jnp.where(done[None, None], new_scores, -1e30)
    top = jnp.maximum(
        jnp.max(cache_scores, axis=(1, 3)), jnp.max(new_scores, axis=-1)
    )
    cache_exp = jnp.exp(cache_scores - top[:, None, :, None, :])
    new_exp = jnp.exp(new_scores - top[..., None])
    total = jnp.sum(cache_exp, axis=(1, 3)) + jnp.sum(new_exp, axis=-1)
    cache_w = (cache_exp / total[:, None, :, None, :]).astype(jnp.bfloat16)
    new_w = (new_exp / total[..., None]).astype(jnp.bfloat16)
    attended = jnp.einsum(
        "rjgpx,rjgpd->rjgxd", cache_w, values, preferred_element_type=jnp.float32
    ).sum(axis=1)
    attended = attended + jnp.einsum(
        "rgxs,rgsd->rgxd", new_w, fresh, preferred_element_type=jnp.float32
    )
    attended = attended.reshape(reqs, kv_heads, steps, group, head)
    attended = jnp.transpose(attended, (2, 0, 1, 3, 4)).reshape(steps, reqs, width)
    return (wide + scale * attended).astype(jnp.bfloat16)


def per_device(tokens, kv_pool, page_table, lengths, migrate_ids, norm_gain, out_scale):
    inputs = tokens[0]
    pool = kv_pool[0, 0]
    table = page_table[0]
    lens = lengths[0]
    moving = migrate_ids[0]
    gain = norm_gain[0]
    scale = out_scale[0]
    steps, reqs, width = inputs.shape
    page_len = pool.shape[3]
    chosen = table[moving]
    outgoing = pool[chosen]
    spots = jnp.arange(chosen.shape[1])[:, None] * page_len + jnp.arange(page_len)[None, :]
    keep = spots[None, :, :] < lens[moving][:, None, None]
    outgoing = jnp.where(keep[:, :, None, None, :, None], outgoing, jnp.zeros((), jnp.bfloat16))
    received = partner(outgoing, "inst", 0)
    flat_pool = pool.reshape((-1,) + pool.shape[2:])
    keys = flat_pool[table * 2]
    values = flat_pool[table * 2 + 1]
    lens_used = lens
    section = lax.axis_index("section")
    count = lax.axis_size("section")
    chunks = CHUNKS
    block = reqs // chunks

    incoming = jnp.zeros((steps, block, width), jnp.bfloat16)
    finished = jnp.zeros((steps, reqs, width), jnp.bfloat16)
    zero = jnp.zeros((), jnp.int32)
    for k in range(chunks + count - 1):
        item = k - section
        live = jnp.logical_and(item >= 0, item < chunks)
        start = jnp.clip(item, 0, chunks - 1) * block
        if k > 0:
            start, incoming = lax.optimization_barrier((start, incoming))
        first = lax.dynamic_slice_in_dim(inputs, start, block, 1)
        rows = jnp.where(section == 0, first, incoming)
        part_keys = lax.dynamic_slice_in_dim(keys, start, block, 0)
        part_values = lax.dynamic_slice_in_dim(values, start, block, 0)
        part_lens = lax.dynamic_slice_in_dim(lens_used, start, block, 0)
        result = layer(rows, part_keys, part_values, part_lens, gain, scale)
        previous = lax.dynamic_slice_in_dim(finished, start, block, 1)
        finished = lax.dynamic_update_slice(
            finished, jnp.where(live, result, previous), (zero, start, zero)
        )
        pairs = [(s, s + 1) for s in range(count - 1) if 0 <= k - s < chunks]
        if pairs:
            incoming = lax.ppermute(result, "section", pairs)
    handed = partner(finished[:, moving], "inst", 0)
    finished = finished.at[:, moving].set(handed)
    return (finished[None, None], received[None, None])


def solution(mesh):
    in_specs = (
        P(("groups", "inst"), None, None, None),
        P(("groups", "inst"), "section", None, None, None, None, None),
        P(("groups", "inst"), None, None),
        P(("groups", "inst"), None),
        P(("groups", "inst"), None),
        P("section", None),
        P("section", None),
    )
    out_specs = (
        P(("groups", "inst"), "section", None, None, None),
        P(("groups", "inst"), "section", None, None, None, None, None, None),
    )
    return jax.shard_map(
        per_device, mesh=mesh, in_specs=in_specs, out_specs=out_specs, check_vma=False
    )
```

```python
import math

import jax
import jax.numpy as jnp
from jax import lax
from jax.sharding import PartitionSpec as P

CHUNKS = 4


def partner(block, axis, stride):
    count = lax.axis_size(axis)
    route = []
    for low in range(count):
        high = low | 1 << stride
        if high != low and high < count:
            route += [(low, high), (high, low)]
    return lax.ppermute(block, axis, route)


def passed_along(array, axis, by):
    peers = lax.axis_size(axis)
    pairs = [(i, i + by) for i in range(peers) if 0 <= i + by < peers]
    return lax.ppermute(array, axis, pairs)


def layer(rows, keys, values, lens, gain, scale):
    steps, reqs, width = rows.shape
    pages = keys.shape[1]
    kv_heads = keys.shape[2]
    page_len = keys.shape[3]
    head = keys.shape[4]
    group = width // (kv_heads * head)
    wide = rows.astype(jnp.float32)
    normed = wide * lax.rsqrt(jnp.mean(wide * wide, axis=-1, keepdims=True) + 1e-05) * gain
    heads = normed.reshape(steps, reqs, kv_heads, group, head)
    query = jnp.transpose(heads.astype(jnp.bfloat16), (1, 2, 0, 3, 4))
    query = query.reshape(reqs, kv_heads, steps * group, head)
    fresh = jnp.mean(heads, axis=3).astype(jnp.bfloat16)
    fresh = jnp.transpose(fresh, (1, 2, 0, 3))
    factor = 1.0 / math.sqrt(head)
    wide_query = jnp.broadcast_to(query[:, None], (reqs, pages) + query.shape[1:])
    cache_scores = (
        jnp.einsum("rjgpd,rjgxd->rjgpx", keys, wide_query, preferred_element_type=jnp.float32)
        * factor
    )
    positions = jnp.arange(pages)[:, None] * page_len + jnp.arange(page_len)[None, :]
    live = positions[None] < lens[:, None, None]
    cache_scores = jnp.where(live[:, :, None, :, None], cache_scores, -1e30)
    new_scores = (
        jnp.einsum("rgxd,rgsd->rgxs", query, fresh, preferred_element_type=jnp.float32) * factor
    )
    step_of = jnp.arange(steps * group) // group
    done = jnp.arange(steps)[None, :] <= step_of[:, None]
    new_scores = jnp.where(done[None, None], new_scores, -1e30)
    top = jnp.maximum(
        jnp.max(cache_scores, axis=(1, 3)), jnp.max(new_scores, axis=-1)
    )
    cache_exp = jnp.exp(cache_scores - top[:, None, :, None, :])
    new_exp = jnp.exp(new_scores - top[..., None])
    total = jnp.sum(cache_exp, axis=(1, 3)) + jnp.sum(new_exp, axis=-1)
    cache_w = (cache_exp / total[:, None, :, None, :]).astype(jnp.bfloat16)
    new_w = (new_exp / total[..., None]).astype(jnp.bfloat16)
    attended = jnp.einsum(
        "rjgpx,rjgpd->rjgxd", cache_w, values, preferred_element_type=jnp.float32
    ).sum(axis=1)
    attended = attended + jnp.einsum(
        "rgxs,rgsd->rgxd", new_w, fresh, preferred_element_type=jnp.float32
    )
    attended = attended.reshape(reqs, kv_heads, steps, group, head)
    attended = jnp.transpose(attended, (2, 0, 1, 3, 4)).reshape(steps, reqs, width)
    return (wide + scale * attended).astype(jnp.bfloat16)


def per_device(tokens, kv_pool, page_table, lengths, migrate_ids, norm_gain, out_scale):
    inputs = tokens[0]
    pool = kv_pool[0, 0]
    table = page_table[0]
    lens = lengths[0]
    moving = migrate_ids[0]
    gain = norm_gain[0]
    scale = out_scale[0]
    steps, reqs, width = inputs.shape
    page_len = pool.shape[3]
    chosen = table[moving]
    outgoing = pool[chosen]
    spots = jnp.arange(chosen.shape[1])[:, None] * page_len + jnp.arange(page_len)[None, :]
    keep = spots[None, :, :] < lens[moving][:, None, None]
    outgoing = jnp.where(keep[:, :, None, None, :, None], outgoing, jnp.zeros((), jnp.bfloat16))
    received = partner(outgoing, "inst", 0)
    flat_pool = pool.reshape((-1,) + pool.shape[2:])
    keys = flat_pool[table * 2]
    values = flat_pool[table * 2 + 1]
    lens_used = lens
    section = lax.axis_index("section")
    count = lax.axis_size("section")
    chunks = CHUNKS
    block = reqs // chunks

    incoming = jnp.zeros((steps, block, width), jnp.bfloat16)
    finished = jnp.zeros((steps, reqs, width), jnp.bfloat16)
    zero = jnp.zeros((), jnp.int32)
    for k in range(chunks + count - 1):
        item = k - section
        live = jnp.logical_and(item >= 0, item < chunks)
        start = jnp.clip(item, 0, chunks - 1) * block
        if k > 0:
            start, incoming = lax.optimization_barrier((start, incoming))
        first = lax.dynamic_slice_in_dim(inputs, start, block, 1)
        rows = jnp.where(section == 0, first, incoming)
        part_keys = lax.dynamic_slice_in_dim(keys, start, block, 0)
        part_values = lax.dynamic_slice_in_dim(values, start, block, 0)
        part_lens = lax.dynamic_slice_in_dim(lens_used, start, block, 0)
        result = layer(rows, part_keys, part_values, part_lens, gain, scale)
        previous = lax.dynamic_slice_in_dim(finished, start, block, 1)
        finished = lax.dynamic_update_slice(
            finished, jnp.where(live, result, previous), (zero, start, zero)
        )
        pairs = [(s, s + 1) for s in range(count - 1) if 0 <= k - s < chunks]
        even = [pair for pair in pairs if pair[0] % 2 == 0]
        odd = [pair for pair in pairs if pair[0] % 2 == 1]
        if even and odd:
            from_even = lax.ppermute(result, "section", even)
            from_odd = lax.ppermute(result, "section", odd)
            incoming = jnp.where(section % 2 == 1, from_even, from_odd)
        elif pairs:
            incoming = lax.ppermute(result, "section", pairs)
    handed = partner(finished[:, moving], "inst", 0)
    finished = finished.at[:, moving].set(handed)
    return (finished[None, None], received[None, None])


def solution(mesh):
    in_specs = (
        P(("groups", "inst"), None, None, None),
        P(("groups", "inst"), "section", None, None, None, None, None),
        P(("groups", "inst"), None, None),
        P(("groups", "inst"), None),
        P(("groups", "inst"), None),
        P("section", None),
        P("section", None),
    )
    out_specs = (
        P(("groups", "inst"), "section", None, None, None),
        P(("groups", "inst"), "section", None, None, None, None, None, None),
    )
    return jax.shard_map(
        per_device, mesh=mesh, in_specs=in_specs, out_specs=out_specs, check_vma=False
    )
```

```python
import math

import jax
import jax.numpy as jnp
from jax import lax
from jax.sharding import PartitionSpec as P
from jax.experimental import pallas as pl
from jax.experimental.pallas import tpu as pltpu

CHUNKS = 4


def partner(block, axis, stride):
    count = lax.axis_size(axis)
    route = []
    for low in range(count):
        high = low | 1 << stride
        if high != low and high < count:
            route += [(low, high), (high, low)]
    return lax.ppermute(block, axis, route)


def passed_along(array, axis, by):
    peers = lax.axis_size(axis)
    pairs = [(i, i + by) for i in range(peers) if 0 <= i + by < peers]
    return lax.ppermute(array, axis, pairs)


def layer(rows, keys, values, lens, gain, scale):
    steps, reqs, width = rows.shape
    pages = keys.shape[1]
    kv_heads = keys.shape[2]
    page_len = keys.shape[3]
    head = keys.shape[4]
    group = width // (kv_heads * head)
    wide = rows.astype(jnp.float32)
    normed = wide * lax.rsqrt(jnp.mean(wide * wide, axis=-1, keepdims=True) + 1e-05) * gain
    heads = normed.reshape(steps, reqs, kv_heads, group, head)
    query = jnp.transpose(heads.astype(jnp.bfloat16), (1, 2, 0, 3, 4))
    query = query.reshape(reqs, kv_heads, steps * group, head)
    fresh = jnp.mean(heads, axis=3).astype(jnp.bfloat16)
    fresh = jnp.transpose(fresh, (1, 2, 0, 3))
    factor = 1.0 / math.sqrt(head)
    wide_query = jnp.broadcast_to(query[:, None], (reqs, pages) + query.shape[1:])
    cache_scores = (
        jnp.einsum("rjgxd,rjgpd->rjgxp", wide_query, keys, preferred_element_type=jnp.float32)
        * factor
    )
    positions = jnp.arange(pages)[:, None] * page_len + jnp.arange(page_len)[None, :]
    live = positions[None] < lens[:, None, None]
    cache_scores = jnp.where(live[:, :, None, None, :], cache_scores, -1e30)
    new_scores = (
        jnp.einsum("rgxd,rgsd->rgxs", query, fresh, preferred_element_type=jnp.float32) * factor
    )
    step_of = jnp.arange(steps * group) // group
    done = jnp.arange(steps)[None, :] <= step_of[:, None]
    new_scores = jnp.where(done[None, None], new_scores, -1e30)
    top = jnp.maximum(
        jnp.max(cache_scores, axis=(1, 4)), jnp.max(new_scores, axis=-1)
    )[..., None]
    cache_exp = jnp.exp(cache_scores - top[:, None])
    new_exp = jnp.exp(new_scores - top)
    total = jnp.sum(cache_exp, axis=(1, 4))[..., None] + jnp.sum(new_exp, axis=-1, keepdims=True)
    cache_w = (cache_exp / total[:, None]).astype(jnp.bfloat16)
    new_w = (new_exp / total).astype(jnp.bfloat16)
    attended = jnp.einsum(
        "rjgxp,rjgpd->rjgxd", cache_w, values, preferred_element_type=jnp.float32
    ).sum(axis=1)
    attended = attended + jnp.einsum(
        "rgxs,rgsd->rgxd", new_w, fresh, preferred_element_type=jnp.float32
    )
    attended = attended.reshape(reqs, kv_heads, steps, group, head)
    attended = jnp.transpose(attended, (2, 0, 1, 3, 4)).reshape(steps, reqs, width)
    return (wide + scale * attended).astype(jnp.bfloat16)


def attend_kernel(table_ref, lens_ref, start_ref, q_ref, f_ref, *refs):
    pages = (len(refs) - 1) // 2
    key_refs = refs[:pages]
    value_refs = refs[pages:2 * pages]
    o_ref = refs[-1]
    req = start_ref[0] + pl.program_id(0)
    length = lens_ref[req]
    query = q_ref[0]
    kv_heads, rows, head = query.shape
    fresh = f_ref[0].astype(jnp.float32)
    steps = fresh.shape[1]
    group = rows // steps
    page_len = key_refs[0].shape[3]
    factor = 1.0 / math.sqrt(head)
    spots = lax.broadcasted_iota(jnp.int32, (kv_heads, rows, page_len), 2)
    scores = []
    for j in range(pages):
        got = lax.dot_general(
            query, key_refs[j][0, 0], (((2,), (2,)), ((0,), (0,))),
            preferred_element_type=jnp.float32,
        ) * factor
        scores.append(jnp.where(spots + j * page_len < length, got, -1e30))
    wide_query = query.astype(jnp.float32)
    step_of = lax.broadcasted_iota(jnp.int32, (kv_heads, rows), 1) // group
    news = []
    for s in range(steps):
        got = jnp.sum(wide_query * fresh[:, s][:, None, :], axis=-1) * factor
        news.append(jnp.where(step_of >= s, got, -1e30))
    top = jnp.max(scores[0], axis=-1)
    for j in range(1, pages):
        top = jnp.maximum(top, jnp.max(scores[j], axis=-1))
    for s in range(steps):
        top = jnp.maximum(top, news[s])
    exps = [jnp.exp(x - top[..., None]) for x in scores]
    new_exps = [jnp.exp(x - top) for x in news]
    total = sum(jnp.sum(x, axis=-1) for x in exps) + sum(new_exps)
    out = None
    for j in range(pages):
        weight = (exps[j] / total[..., None]).astype(jnp.bfloat16)
        part = lax.dot_general(
            weight, value_refs[j][0, 0], (((2,), (1,)), ((0,), (0,))),
            preferred_element_type=jnp.float32,
        )
        out = part if out is None else out + part
    for s in range(steps):
        weight = (new_exps[s] / total).astype(jnp.bfloat16).astype(jnp.float32)
        out = out + weight[..., None] * fresh[:, s][:, None, :]
    o_ref[0] = out


def attend(query, fresh, pool, table, lens, start):
    reqs, kv_heads, rows, head = query.shape
    steps = fresh.shape[2]
    pages = table.shape[1]
    page_len = pool.shape[3]
    flat = table.reshape(-1)

    def page_spec(j, half):
        def index(r, table_ref, lens_ref, start_ref):
            return (table_ref[(start_ref[0] + r) * pages + j], half, 0, 0, 0)

        return pl.BlockSpec((1, 1, kv_heads, page_len, head), index)

    def row_spec(width):
        return pl.BlockSpec((1, kv_heads, width, head), lambda r, *_: (r, 0, 0, 0))

    grid_spec = pltpu.PrefetchScalarGridSpec(
        num_scalar_prefetch=3,
        grid=(reqs,),
        in_specs=[row_spec(rows), row_spec(steps)]
        + [page_spec(j, 0) for j in range(pages)]
        + [page_spec(j, 1) for j in range(pages)],
        out_specs=row_spec(rows),
    )
    return pl.pallas_call(
        attend_kernel,
        grid_spec=grid_spec,
        out_shape=jax.ShapeDtypeStruct(query.shape, jnp.float32),
    )(flat, lens, start.reshape(1), query, fresh, *([pool] * (2 * pages)))


def layer_paged(rows, pool, table, lens, start, gain, scale):
    steps, reqs, width = rows.shape
    kv_heads = pool.shape[2]
    head = pool.shape[4]
    group = width // (kv_heads * head)
    wide = rows.astype(jnp.float32)
    normed = wide * lax.rsqrt(jnp.mean(wide * wide, axis=-1, keepdims=True) + 1e-05) * gain
    heads = normed.reshape(steps, reqs, kv_heads, group, head)
    query = jnp.transpose(heads.astype(jnp.bfloat16), (1, 2, 0, 3, 4))
    query = query.reshape(reqs, kv_heads, steps * group, head)
    fresh = jnp.mean(heads, axis=3).astype(jnp.bfloat16)
    fresh = jnp.transpose(fresh, (1, 2, 0, 3))
    attended = attend(query, fresh, pool, table, lens, start)
    attended = attended.reshape(reqs, kv_heads, steps, group, head)
    attended = jnp.transpose(attended, (2, 0, 1, 3, 4)).reshape(steps, reqs, width)
    return (wide + scale * attended).astype(jnp.bfloat16)


def per_device(tokens, kv_pool, page_table, lengths, migrate_ids, norm_gain, out_scale):
    inputs = tokens[0]
    pool = kv_pool[0, 0]
    table = page_table[0]
    lens = lengths[0]
    moving = migrate_ids[0]
    gain = norm_gain[0]
    scale = out_scale[0]
    steps, reqs, width = inputs.shape
    page_len = pool.shape[3]
    chosen = table[moving]
    outgoing = pool[chosen]
    spots = jnp.arange(chosen.shape[1])[:, None] * page_len + jnp.arange(page_len)[None, :]
    keep = spots[None, :, :] < lens[moving][:, None, None]
    outgoing = jnp.where(keep[:, :, None, None, :, None], outgoing, jnp.zeros((), jnp.bfloat16))
    received = partner(outgoing, "inst", 0)
    lens_used = lens
    section = lax.axis_index("section")
    count = lax.axis_size("section")
    chunks = CHUNKS
    block = reqs // chunks

    incoming = jnp.zeros((steps, block, width), jnp.bfloat16)
    finished = jnp.zeros((steps, reqs, width), jnp.bfloat16)
    zero = jnp.zeros((), jnp.int32)
    for k in range(chunks + count - 1):
        item = k - section
        live = jnp.logical_and(item >= 0, item < chunks)
        start = jnp.clip(item, 0, chunks - 1) * block
        if k > 0:
            start, incoming = lax.optimization_barrier((start, incoming))
        first = lax.dynamic_slice_in_dim(inputs, start, block, 1)
        rows = jnp.where(section == 0, first, incoming)
        result = layer_paged(rows, pool, table, lens_used, start, gain, scale)
        previous = lax.dynamic_slice_in_dim(finished, start, block, 1)
        finished = lax.dynamic_update_slice(
            finished, jnp.where(live, result, previous), (zero, start, zero)
        )
        pairs = [(s, s + 1) for s in range(count - 1) if 0 <= k - s < chunks]
        if pairs:
            incoming = lax.ppermute(result, "section", pairs)
    handed = partner(finished[:, moving], "inst", 0)
    finished = finished.at[:, moving].set(handed)
    return (finished[None, None], received[None, None])


def solution(mesh):
    in_specs = (
        P(("groups", "inst"), None, None, None),
        P(("groups", "inst"), "section", None, None, None, None, None),
        P(("groups", "inst"), None, None),
        P(("groups", "inst"), None),
        P(("groups", "inst"), None),
        P("section", None),
        P("section", None),
    )
    out_specs = (
        P(("groups", "inst"), "section", None, None, None),
        P(("groups", "inst"), "section", None, None, None, None, None, None),
    )
    return jax.shard_map(
        per_device, mesh=mesh, in_specs=in_specs, out_specs=out_specs, check_vma=False
    )
```

```python
import math

import jax
import jax.numpy as jnp
from jax import lax
from jax.sharding import PartitionSpec as P
from jax.experimental import pallas as pl
from jax.experimental.pallas import tpu as pltpu

CHUNKS = 4


def partner(block, axis, stride):
    count = lax.axis_size(axis)
    route = []
    for low in range(count):
        high = low | 1 << stride
        if high != low and high < count:
            route += [(low, high), (high, low)]
    return lax.ppermute(block, axis, route)


def passed_along(array, axis, by):
    peers = lax.axis_size(axis)
    pairs = [(i, i + by) for i in range(peers) if 0 <= i + by < peers]
    return lax.ppermute(array, axis, pairs)


def layer(rows, keys, values, lens, gain, scale):
    steps, reqs, width = rows.shape
    pages = keys.shape[1]
    kv_heads = keys.shape[2]
    page_len = keys.shape[3]
    head = keys.shape[4]
    group = width // (kv_heads * head)
    wide = rows.astype(jnp.float32)
    normed = wide * lax.rsqrt(jnp.mean(wide * wide, axis=-1, keepdims=True) + 1e-05) * gain
    heads = normed.reshape(steps, reqs, kv_heads, group, head)
    query = jnp.transpose(heads.astype(jnp.bfloat16), (1, 2, 0, 3, 4))
    query = query.reshape(reqs, kv_heads, steps * group, head)
    fresh = jnp.mean(heads, axis=3).astype(jnp.bfloat16)
    fresh = jnp.transpose(fresh, (1, 2, 0, 3))
    factor = 1.0 / math.sqrt(head)
    wide_query = jnp.broadcast_to(query[:, None], (reqs, pages) + query.shape[1:])
    cache_scores = (
        jnp.einsum("rjgxd,rjgpd->rjgxp", wide_query, keys, preferred_element_type=jnp.float32)
        * factor
    )
    positions = jnp.arange(pages)[:, None] * page_len + jnp.arange(page_len)[None, :]
    live = positions[None] < lens[:, None, None]
    cache_scores = jnp.where(live[:, :, None, None, :], cache_scores, -1e30)
    new_scores = (
        jnp.einsum("rgxd,rgsd->rgxs", query, fresh, preferred_element_type=jnp.float32) * factor
    )
    step_of = jnp.arange(steps * group) // group
    done = jnp.arange(steps)[None, :] <= step_of[:, None]
    new_scores = jnp.where(done[None, None], new_scores, -1e30)
    top = jnp.maximum(
        jnp.max(cache_scores, axis=(1, 4)), jnp.max(new_scores, axis=-1)
    )[..., None]
    cache_exp = jnp.exp(cache_scores - top[:, None])
    new_exp = jnp.exp(new_scores - top)
    total = jnp.sum(cache_exp, axis=(1, 4))[..., None] + jnp.sum(new_exp, axis=-1, keepdims=True)
    cache_w = (cache_exp / total[:, None]).astype(jnp.bfloat16)
    new_w = (new_exp / total).astype(jnp.bfloat16)
    attended = jnp.einsum(
        "rjgxp,rjgpd->rjgxd", cache_w, values, preferred_element_type=jnp.float32
    ).sum(axis=1)
    attended = attended + jnp.einsum(
        "rgxs,rgsd->rgxd", new_w, fresh, preferred_element_type=jnp.float32
    )
    attended = attended.reshape(reqs, kv_heads, steps, group, head)
    attended = jnp.transpose(attended, (2, 0, 1, 3, 4)).reshape(steps, reqs, width)
    return (wide + scale * attended).astype(jnp.bfloat16)


def copy_kernel(table_ref, page_ref, keys_ref, values_ref):
    keys_ref[0, 0] = page_ref[0, 0]
    values_ref[0, 0] = page_ref[0, 1]


def gather_pages(pool, table):
    reqs, pages = table.shape
    kv_heads, page_len, head = pool.shape[2:]

    def page_index(r, j, table_ref):
        return (table_ref[r * pages + j], 0, 0, 0, 0)

    def slot_index(r, j, table_ref):
        return (r, j, 0, 0, 0)

    slot = pl.BlockSpec((1, 1, kv_heads, page_len, head), slot_index)
    grid_spec = pltpu.PrefetchScalarGridSpec(
        num_scalar_prefetch=1,
        grid=(reqs, pages),
        in_specs=[pl.BlockSpec((1, 2, kv_heads, page_len, head), page_index)],
        out_specs=[slot, slot],
    )
    half = jax.ShapeDtypeStruct((reqs, pages, kv_heads, page_len, head), pool.dtype)
    return pl.pallas_call(copy_kernel, grid_spec=grid_spec, out_shape=[half, half])(
        table.reshape(-1), pool
    )


def per_device(tokens, kv_pool, page_table, lengths, migrate_ids, norm_gain, out_scale):
    inputs = tokens[0]
    pool = kv_pool[0, 0]
    table = page_table[0]
    lens = lengths[0]
    moving = migrate_ids[0]
    gain = norm_gain[0]
    scale = out_scale[0]
    steps, reqs, width = inputs.shape
    page_len = pool.shape[3]
    chosen = table[moving]
    outgoing = pool[chosen]
    spots = jnp.arange(chosen.shape[1])[:, None] * page_len + jnp.arange(page_len)[None, :]
    keep = spots[None, :, :] < lens[moving][:, None, None]
    outgoing = jnp.where(keep[:, :, None, None, :, None], outgoing, jnp.zeros((), jnp.bfloat16))
    received = partner(outgoing, "inst", 0)
    keys, values = gather_pages(pool, table)
    lens_used = lens
    section = lax.axis_index("section")
    count = lax.axis_size("section")
    chunks = CHUNKS
    block = reqs // chunks

    incoming = jnp.zeros((steps, block, width), jnp.bfloat16)
    finished = jnp.zeros((steps, reqs, width), jnp.bfloat16)
    zero = jnp.zeros((), jnp.int32)
    for k in range(chunks + count - 1):
        item = k - section
        live = jnp.logical_and(item >= 0, item < chunks)
        start = jnp.clip(item, 0, chunks - 1) * block
        if k > 0:
            start, incoming = lax.optimization_barrier((start, incoming))
        first = lax.dynamic_slice_in_dim(inputs, start, block, 1)
        rows = jnp.where(section == 0, first, incoming)
        part_keys = lax.dynamic_slice_in_dim(keys, start, block, 0)
        part_values = lax.dynamic_slice_in_dim(values, start, block, 0)
        part_lens = lax.dynamic_slice_in_dim(lens_used, start, block, 0)
        result = layer(rows, part_keys, part_values, part_lens, gain, scale)
        previous = lax.dynamic_slice_in_dim(finished, start, block, 1)
        finished = lax.dynamic_update_slice(
            finished, jnp.where(live, result, previous), (zero, start, zero)
        )
        pairs = [(s, s + 1) for s in range(count - 1) if 0 <= k - s < chunks]
        if pairs:
            incoming = lax.ppermute(result, "section", pairs)
    handed = partner(finished[:, moving], "inst", 0)
    finished = finished.at[:, moving].set(handed)
    return (finished[None, None], received[None, None])


def solution(mesh):
    in_specs = (
        P(("groups", "inst"), None, None, None),
        P(("groups", "inst"), "section", None, None, None, None, None),
        P(("groups", "inst"), None, None),
        P(("groups", "inst"), None),
        P(("groups", "inst"), None),
        P("section", None),
        P("section", None),
    )
    out_specs = (
        P(("groups", "inst"), "section", None, None, None),
        P(("groups", "inst"), "section", None, None, None, None, None, None),
    )
    return jax.shard_map(
        per_device, mesh=mesh, in_specs=in_specs, out_specs=out_specs, check_vma=False
    )
```

```python
import math

import jax
import jax.numpy as jnp
from jax import lax
from jax.sharding import PartitionSpec as P
from jax.experimental import pallas as pl
from jax.experimental.pallas import tpu as pltpu

CHUNKS = 4


def partner(block, axis, stride):
    count = lax.axis_size(axis)
    route = []
    for low in range(count):
        high = low | 1 << stride
        if high != low and high < count:
            route += [(low, high), (high, low)]
    return lax.ppermute(block, axis, route)


def passed_along(array, axis, by):
    peers = lax.axis_size(axis)
    pairs = [(i, i + by) for i in range(peers) if 0 <= i + by < peers]
    return lax.ppermute(array, axis, pairs)


def layer(rows, keys, values, lens, gain, scale):
    steps, reqs, width = rows.shape
    pages = keys.shape[1]
    kv_heads = keys.shape[2]
    page_len = keys.shape[3]
    head = keys.shape[4]
    group = width // (kv_heads * head)
    wide = rows.astype(jnp.float32)
    normed = wide * lax.rsqrt(jnp.mean(wide * wide, axis=-1, keepdims=True) + 1e-05) * gain
    heads = normed.reshape(steps, reqs, kv_heads, group, head)
    query = jnp.transpose(heads.astype(jnp.bfloat16), (1, 2, 0, 3, 4))
    query = query.reshape(reqs, kv_heads, steps * group, head)
    fresh = jnp.mean(heads, axis=3).astype(jnp.bfloat16)
    fresh = jnp.transpose(fresh, (1, 2, 0, 3))
    factor = 1.0 / math.sqrt(head)
    wide_query = jnp.broadcast_to(query[:, None], (reqs, pages) + query.shape[1:])
    cache_scores = (
        jnp.einsum("rjgxd,rjgpd->rjgxp", wide_query, keys, preferred_element_type=jnp.float32)
        * factor
    )
    positions = jnp.arange(pages)[:, None] * page_len + jnp.arange(page_len)[None, :]
    live = positions[None] < lens[:, None, None]
    cache_scores = jnp.where(live[:, :, None, None, :], cache_scores, -1e30)
    new_scores = (
        jnp.einsum("rgxd,rgsd->rgxs", query, fresh, preferred_element_type=jnp.float32) * factor
    )
    step_of = jnp.arange(steps * group) // group
    done = jnp.arange(steps)[None, :] <= step_of[:, None]
    new_scores = jnp.where(done[None, None], new_scores, -1e30)
    top = jnp.maximum(
        jnp.max(cache_scores, axis=(1, 4)), jnp.max(new_scores, axis=-1)
    )[..., None]
    cache_exp = jnp.exp(cache_scores - top[:, None])
    new_exp = jnp.exp(new_scores - top)
    total = jnp.sum(cache_exp, axis=(1, 4))[..., None] + jnp.sum(new_exp, axis=-1, keepdims=True)
    cache_w = (cache_exp / total[:, None]).astype(jnp.bfloat16)
    new_w = (new_exp / total).astype(jnp.bfloat16)
    attended = jnp.einsum(
        "rjgxp,rjgpd->rjgxd", cache_w, values, preferred_element_type=jnp.float32
    ).sum(axis=1)
    attended = attended + jnp.einsum(
        "rgxs,rgsd->rgxd", new_w, fresh, preferred_element_type=jnp.float32
    )
    attended = attended.reshape(reqs, kv_heads, steps, group, head)
    attended = jnp.transpose(attended, (2, 0, 1, 3, 4)).reshape(steps, reqs, width)
    return (wide + scale * attended).astype(jnp.bfloat16)


def copy_kernel(table_ref, page_ref, *refs):
    keys_ref, values_ref = refs[-2], refs[-1]
    keys_ref[0, 0] = page_ref[0, 0]
    values_ref[0, 0] = page_ref[0, 1]


def gather_chunk(pool, table, chunk, block, previous):
    reqs, pages = table.shape
    kv_heads, page_len, head = pool.shape[2:]

    def page_index(r, j, table_ref):
        return (table_ref[(chunk * block + r) * pages + j], 0, 0, 0, 0)

    def slot_index(r, j, table_ref):
        return (chunk * block + r, j, 0, 0, 0)

    slot = pl.BlockSpec((1, 1, kv_heads, page_len, head), slot_index)
    in_specs = [pl.BlockSpec((1, 2, kv_heads, page_len, head), page_index)]
    operands = [table.reshape(-1), pool]
    aliases = {}
    if previous is not None:
        in_specs += [pl.BlockSpec(memory_space=pl.ANY)] * 2
        operands += list(previous)
        aliases = {2: 0, 3: 1}
    grid_spec = pltpu.PrefetchScalarGridSpec(
        num_scalar_prefetch=1,
        grid=(block, pages),
        in_specs=in_specs,
        out_specs=[slot, slot],
    )
    half = jax.ShapeDtypeStruct((reqs, pages, kv_heads, page_len, head), pool.dtype)
    return pl.pallas_call(
        copy_kernel, grid_spec=grid_spec, out_shape=[half, half], input_output_aliases=aliases
    )(*operands)

def per_device(tokens, kv_pool, page_table, lengths, migrate_ids, norm_gain, out_scale):
    inputs = tokens[0]
    pool = kv_pool[0, 0]
    table = page_table[0]
    lens = lengths[0]
    moving = migrate_ids[0]
    gain = norm_gain[0]
    scale = out_scale[0]
    steps, reqs, width = inputs.shape
    page_len = pool.shape[3]
    chosen = table[moving]
    outgoing = pool[chosen]
    spots = jnp.arange(chosen.shape[1])[:, None] * page_len + jnp.arange(page_len)[None, :]
    keep = spots[None, :, :] < lens[moving][:, None, None]
    outgoing = jnp.where(keep[:, :, None, None, :, None], outgoing, jnp.zeros((), jnp.bfloat16))
    received = partner(outgoing, "inst", 0)
    lens_used = lens
    section = lax.axis_index("section")
    count = lax.axis_size("section")
    chunks = CHUNKS
    block = reqs // chunks

    incoming = jnp.zeros((steps, block, width), jnp.bfloat16)
    finished = jnp.zeros((steps, reqs, width), jnp.bfloat16)
    zero = jnp.zeros((), jnp.int32)
    keys, values = None, None
    for k in range(chunks + count - 1):
        if k < chunks:
            previous = None if keys is None else (keys, values)
            keys, values = gather_chunk(pool, table, k, block, previous)
        item = k - section
        live = jnp.logical_and(item >= 0, item < chunks)
        start = jnp.clip(item, 0, chunks - 1) * block
        if k > 0:
            start, incoming = lax.optimization_barrier((start, incoming))
        first = lax.dynamic_slice_in_dim(inputs, start, block, 1)
        rows = jnp.where(section == 0, first, incoming)
        part_keys = lax.dynamic_slice_in_dim(keys, start, block, 0)
        part_values = lax.dynamic_slice_in_dim(values, start, block, 0)
        part_lens = lax.dynamic_slice_in_dim(lens_used, start, block, 0)
        result = layer(rows, part_keys, part_values, part_lens, gain, scale)
        previous = lax.dynamic_slice_in_dim(finished, start, block, 1)
        finished = lax.dynamic_update_slice(
            finished, jnp.where(live, result, previous), (zero, start, zero)
        )
        pairs = [(s, s + 1) for s in range(count - 1) if 0 <= k - s < chunks]
        if pairs:
            incoming = lax.ppermute(result, "section", pairs)
    handed = partner(finished[:, moving], "inst", 0)
    finished = finished.at[:, moving].set(handed)
    return (finished[None, None], received[None, None])


def solution(mesh):
    in_specs = (
        P(("groups", "inst"), None, None, None),
        P(("groups", "inst"), "section", None, None, None, None, None),
        P(("groups", "inst"), None, None),
        P(("groups", "inst"), None),
        P(("groups", "inst"), None),
        P("section", None),
        P("section", None),
    )
    out_specs = (
        P(("groups", "inst"), "section", None, None, None),
        P(("groups", "inst"), "section", None, None, None, None, None, None),
    )
    return jax.shard_map(
        per_device, mesh=mesh, in_specs=in_specs, out_specs=out_specs, check_vma=False
    )
```

```python
import math

import jax
import jax.numpy as jnp
from jax import lax
from jax.sharding import PartitionSpec as P
from jax.experimental import pallas as pl
from jax.experimental.pallas import tpu as pltpu

CHUNKS = 4


def partner(block, axis, stride):
    count = lax.axis_size(axis)
    route = []
    for low in range(count):
        high = low | 1 << stride
        if high != low and high < count:
            route += [(low, high), (high, low)]
    return lax.ppermute(block, axis, route)


def passed_along(array, axis, by):
    peers = lax.axis_size(axis)
    pairs = [(i, i + by) for i in range(peers) if 0 <= i + by < peers]
    return lax.ppermute(array, axis, pairs)


def layer(rows, keys, values, lens, gain, scale):
    steps, reqs, width = rows.shape
    pages = keys.shape[1]
    kv_heads = keys.shape[2]
    page_len = keys.shape[3]
    head = keys.shape[4]
    group = width // (kv_heads * head)
    wide = rows.astype(jnp.float32)
    normed = wide * lax.rsqrt(jnp.mean(wide * wide, axis=-1, keepdims=True) + 1e-05) * gain
    heads = normed.reshape(steps, reqs, kv_heads, group, head)
    query = jnp.transpose(heads.astype(jnp.bfloat16), (1, 2, 0, 3, 4))
    query = query.reshape(reqs, kv_heads, steps * group, head)
    fresh = jnp.mean(heads, axis=3).astype(jnp.bfloat16)
    fresh = jnp.transpose(fresh, (1, 2, 0, 3))
    factor = 1.0 / math.sqrt(head)
    wide_query = jnp.broadcast_to(query[:, None], (reqs, pages) + query.shape[1:])
    cache_scores = (
        jnp.einsum("rjgxd,rjgpd->rjgxp", wide_query, keys, preferred_element_type=jnp.float32)
        * factor
    )
    positions = jnp.arange(pages)[:, None] * page_len + jnp.arange(page_len)[None, :]
    live = positions[None] < lens[:, None, None]
    cache_scores = jnp.where(live[:, :, None, None, :], cache_scores, -1e30)
    new_scores = (
        jnp.einsum("rgxd,rgsd->rgxs", query, fresh, preferred_element_type=jnp.float32) * factor
    )
    step_of = jnp.arange(steps * group) // group
    done = jnp.arange(steps)[None, :] <= step_of[:, None]
    new_scores = jnp.where(done[None, None], new_scores, -1e30)
    top = jnp.maximum(
        jnp.max(cache_scores, axis=(1, 4)), jnp.max(new_scores, axis=-1)
    )[..., None]
    cache_exp = jnp.exp(cache_scores - top[:, None])
    new_exp = jnp.exp(new_scores - top)
    total = jnp.sum(cache_exp, axis=(1, 4))[..., None] + jnp.sum(new_exp, axis=-1, keepdims=True)
    cache_w = (cache_exp / total[:, None]).astype(jnp.bfloat16)
    new_w = (new_exp / total).astype(jnp.bfloat16)
    attended = jnp.einsum(
        "rjgxp,rjgpd->rjgxd", cache_w, values, preferred_element_type=jnp.float32
    ).sum(axis=1)
    attended = attended + jnp.einsum(
        "rgxs,rgsd->rgxd", new_w, fresh, preferred_element_type=jnp.float32
    )
    attended = attended.reshape(reqs, kv_heads, steps, group, head)
    attended = jnp.transpose(attended, (2, 0, 1, 3, 4)).reshape(steps, reqs, width)
    return (wide + scale * attended).astype(jnp.bfloat16)


def copy_kernel(table_ref, page_ref, *refs):
    keys_ref, values_ref = refs[-2], refs[-1]
    keys_ref[0, 0] = page_ref[0, 0]
    values_ref[0, 0] = page_ref[0, 1]


def gather_chunk(pool, table, chunk, block, previous):
    reqs, pages = table.shape
    kv_heads, page_len, head = pool.shape[2:]

    def page_index(r, j, table_ref):
        return (table_ref[(chunk * block + r) * pages + j], 0, 0, 0, 0)

    def slot_index(r, j, table_ref):
        return (chunk * block + r, j, 0, 0, 0)

    slot = pl.BlockSpec((1, 1, kv_heads, page_len, head), slot_index)
    in_specs = [pl.BlockSpec((1, 2, kv_heads, page_len, head), page_index)]
    operands = [table.reshape(-1), pool]
    aliases = {}
    if previous is not None:
        in_specs += [pl.BlockSpec(memory_space=pl.ANY)] * 2
        operands += list(previous)
        aliases = {2: 0, 3: 1}
    grid_spec = pltpu.PrefetchScalarGridSpec(
        num_scalar_prefetch=1,
        grid=(block, pages),
        in_specs=in_specs,
        out_specs=[slot, slot],
    )
    half = jax.ShapeDtypeStruct((reqs, pages, kv_heads, page_len, head), pool.dtype)
    return pl.pallas_call(
        copy_kernel, grid_spec=grid_spec, out_shape=[half, half], input_output_aliases=aliases
    )(*operands)

def per_device(tokens, kv_pool, page_table, lengths, migrate_ids, norm_gain, out_scale):
    inputs = tokens[0]
    pool = kv_pool[0, 0]
    table = page_table[0]
    lens = lengths[0]
    moving = migrate_ids[0]
    gain = norm_gain[0]
    scale = out_scale[0]
    steps, reqs, width = inputs.shape
    page_len = pool.shape[3]
    chosen = table[moving]
    spots = jnp.arange(chosen.shape[1])[:, None] * page_len + jnp.arange(page_len)[None, :]
    arrived_lens = partner(lens[moving], "inst", 0)
    lens_used = lens
    section = lax.axis_index("section")
    count = lax.axis_size("section")
    chunks = CHUNKS
    block = reqs // chunks

    incoming = jnp.zeros((steps, block, width), jnp.bfloat16)
    finished = jnp.zeros((steps, reqs, width), jnp.bfloat16)
    zero = jnp.zeros((), jnp.int32)
    keys, values = None, None
    for k in range(chunks + count - 1):
        if k < chunks:
            previous = None if keys is None else (keys, values)
            keys, values = gather_chunk(pool, table, k, block, previous)
        item = k - section
        live = jnp.logical_and(item >= 0, item < chunks)
        start = jnp.clip(item, 0, chunks - 1) * block
        if k == 3:
            start, incoming, chosen = lax.optimization_barrier((start, incoming, chosen))
            received = partner(pool[chosen], "inst", 0)
            keep = spots[None, :, :] < arrived_lens[:, None, None]
            arrived = jnp.where(
                keep[:, :, None, None, :, None], received, jnp.zeros((), jnp.bfloat16)
            )
        elif k == 6:
            start, incoming, arrived = lax.optimization_barrier((start, incoming, arrived))
        elif k > 0:
            start, incoming = lax.optimization_barrier((start, incoming))
        first = lax.dynamic_slice_in_dim(inputs, start, block, 1)
        rows = jnp.where(section == 0, first, incoming)
        part_keys = lax.dynamic_slice_in_dim(keys, start, block, 0)
        part_values = lax.dynamic_slice_in_dim(values, start, block, 0)
        part_lens = lax.dynamic_slice_in_dim(lens_used, start, block, 0)
        result = layer(rows, part_keys, part_values, part_lens, gain, scale)
        previous = lax.dynamic_slice_in_dim(finished, start, block, 1)
        finished = lax.dynamic_update_slice(
            finished, jnp.where(live, result, previous), (zero, start, zero)
        )
        pairs = [(s, s + 1) for s in range(count - 1) if 0 <= k - s < chunks]
        if pairs:
            incoming = lax.ppermute(result, "section", pairs)
    handed = partner(finished[:, moving], "inst", 0)
    finished = finished.at[:, moving].set(handed)
    return (finished[None, None], arrived[None, None])


def solution(mesh):
    in_specs = (
        P(("groups", "inst"), None, None, None),
        P(("groups", "inst"), "section", None, None, None, None, None),
        P(("groups", "inst"), None, None),
        P(("groups", "inst"), None),
        P(("groups", "inst"), None),
        P("section", None),
        P("section", None),
    )
    out_specs = (
        P(("groups", "inst"), "section", None, None, None),
        P(("groups", "inst"), "section", None, None, None, None, None, None),
    )
    return jax.shard_map(
        per_device, mesh=mesh, in_specs=in_specs, out_specs=out_specs, check_vma=False
    )
```

```python
import math

import jax
import jax.numpy as jnp
from jax import lax
from jax.sharding import PartitionSpec as P
from jax.experimental import pallas as pl
from jax.experimental.pallas import tpu as pltpu

CHUNKS = 8


def partner(block, axis, stride):
    count = lax.axis_size(axis)
    route = []
    for low in range(count):
        high = low | 1 << stride
        if high != low and high < count:
            route += [(low, high), (high, low)]
    return lax.ppermute(block, axis, route)


def passed_along(array, axis, by):
    peers = lax.axis_size(axis)
    pairs = [(i, i + by) for i in range(peers) if 0 <= i + by < peers]
    return lax.ppermute(array, axis, pairs)


def layer(rows, keys, values, lens, gain, scale):
    steps, reqs, width = rows.shape
    pages = keys.shape[1]
    kv_heads = keys.shape[2]
    page_len = keys.shape[3]
    head = keys.shape[4]
    group = width // (kv_heads * head)
    wide = rows.astype(jnp.float32)
    normed = wide * lax.rsqrt(jnp.mean(wide * wide, axis=-1, keepdims=True) + 1e-05) * gain
    heads = normed.reshape(steps, reqs, kv_heads, group, head)
    query = jnp.transpose(heads.astype(jnp.bfloat16), (1, 2, 0, 3, 4))
    query = query.reshape(reqs, kv_heads, steps * group, head)
    fresh = jnp.mean(heads, axis=3).astype(jnp.bfloat16)
    fresh = jnp.transpose(fresh, (1, 2, 0, 3))
    factor = 1.0 / math.sqrt(head)
    wide_query = jnp.broadcast_to(query[:, None], (reqs, pages) + query.shape[1:])
    cache_scores = (
        jnp.einsum("rjgxd,rjgpd->rjgxp", wide_query, keys, preferred_element_type=jnp.float32)
        * factor
    )
    positions = jnp.arange(pages)[:, None] * page_len + jnp.arange(page_len)[None, :]
    live = positions[None] < lens[:, None, None]
    cache_scores = jnp.where(live[:, :, None, None, :], cache_scores, -1e30)
    new_scores = (
        jnp.einsum("rgxd,rgsd->rgxs", query, fresh, preferred_element_type=jnp.float32) * factor
    )
    step_of = jnp.arange(steps * group) // group
    done = jnp.arange(steps)[None, :] <= step_of[:, None]
    new_scores = jnp.where(done[None, None], new_scores, -1e30)
    top = jnp.maximum(
        jnp.max(cache_scores, axis=(1, 4)), jnp.max(new_scores, axis=-1)
    )[..., None]
    cache_exp = jnp.exp(cache_scores - top[:, None])
    new_exp = jnp.exp(new_scores - top)
    total = jnp.sum(cache_exp, axis=(1, 4))[..., None] + jnp.sum(new_exp, axis=-1, keepdims=True)
    cache_w = (cache_exp / total[:, None]).astype(jnp.bfloat16)
    new_w = (new_exp / total).astype(jnp.bfloat16)
    attended = jnp.einsum(
        "rjgxp,rjgpd->rjgxd", cache_w, values, preferred_element_type=jnp.float32
    ).sum(axis=1)
    attended = attended + jnp.einsum(
        "rgxs,rgsd->rgxd", new_w, fresh, preferred_element_type=jnp.float32
    )
    attended = attended.reshape(reqs, kv_heads, steps, group, head)
    attended = jnp.transpose(attended, (2, 0, 1, 3, 4)).reshape(steps, reqs, width)
    return (wide + scale * attended).astype(jnp.bfloat16)


def copy_kernel(table_ref, page_ref, *refs):
    keys_ref, values_ref = refs[-2], refs[-1]
    keys_ref[0, 0] = page_ref[0, 0]
    values_ref[0, 0] = page_ref[0, 1]


def gather_chunk(pool, table, chunk, block, previous):
    reqs, pages = table.shape
    kv_heads, page_len, head = pool.shape[2:]

    def page_index(r, j, table_ref):
        return (table_ref[(chunk * block + r) * pages + j], 0, 0, 0, 0)

    def slot_index(r, j, table_ref):
        return (chunk * block + r, j, 0, 0, 0)

    slot = pl.BlockSpec((1, 1, kv_heads, page_len, head), slot_index)
    in_specs = [pl.BlockSpec((1, 2, kv_heads, page_len, head), page_index)]
    operands = [table.reshape(-1), pool]
    aliases = {}
    if previous is not None:
        in_specs += [pl.BlockSpec(memory_space=pl.ANY)] * 2
        operands += list(previous)
        aliases = {2: 0, 3: 1}
    grid_spec = pltpu.PrefetchScalarGridSpec(
        num_scalar_prefetch=1,
        grid=(block, pages),
        in_specs=in_specs,
        out_specs=[slot, slot],
    )
    half = jax.ShapeDtypeStruct((reqs, pages, kv_heads, page_len, head), pool.dtype)
    return pl.pallas_call(
        copy_kernel, grid_spec=grid_spec, out_shape=[half, half], input_output_aliases=aliases
    )(*operands)

def per_device(tokens, kv_pool, page_table, lengths, migrate_ids, norm_gain, out_scale):
    inputs = tokens[0]
    pool = kv_pool[0, 0]
    table = page_table[0]
    lens = lengths[0]
    moving = migrate_ids[0]
    gain = norm_gain[0]
    scale = out_scale[0]
    steps, reqs, width = inputs.shape
    page_len = pool.shape[3]
    chosen = table[moving]
    spots = jnp.arange(chosen.shape[1])[:, None] * page_len + jnp.arange(page_len)[None, :]
    arrived_lens = partner(lens[moving], "inst", 0)
    lens_used = lens
    section = lax.axis_index("section")
    count = lax.axis_size("section")
    chunks = CHUNKS
    block = reqs // chunks

    incoming = jnp.zeros((steps, block, width), jnp.bfloat16)
    finished = jnp.zeros((steps, reqs, width), jnp.bfloat16)
    zero = jnp.zeros((), jnp.int32)
    keys, values = None, None
    for k in range(chunks + count - 1):
        if k < chunks:
            previous = None if keys is None else (keys, values)
            keys, values = gather_chunk(pool, table, k, block, previous)
        item = k - section
        live = jnp.logical_and(item >= 0, item < chunks)
        start = jnp.clip(item, 0, chunks - 1) * block
        if k == 3:
            start, incoming, chosen = lax.optimization_barrier((start, incoming, chosen))
            received = partner(pool[chosen], "inst", 0)
            keep = spots[None, :, :] < arrived_lens[:, None, None]
            arrived = jnp.where(
                keep[:, :, None, None, :, None], received, jnp.zeros((), jnp.bfloat16)
            )
        elif k == 6:
            start, incoming, arrived = lax.optimization_barrier((start, incoming, arrived))
        elif k > 0:
            start, incoming = lax.optimization_barrier((start, incoming))
        first = lax.dynamic_slice_in_dim(inputs, start, block, 1)
        rows = jnp.where(section == 0, first, incoming)
        part_keys = lax.dynamic_slice_in_dim(keys, start, block, 0)
        part_values = lax.dynamic_slice_in_dim(values, start, block, 0)
        part_lens = lax.dynamic_slice_in_dim(lens_used, start, block, 0)
        result = layer(rows, part_keys, part_values, part_lens, gain, scale)
        previous = lax.dynamic_slice_in_dim(finished, start, block, 1)
        finished = lax.dynamic_update_slice(
            finished, jnp.where(live, result, previous), (zero, start, zero)
        )
        pairs = [(s, s + 1) for s in range(count - 1) if 0 <= k - s < chunks]
        if pairs:
            incoming = lax.ppermute(result, "section", pairs)
    handed = partner(finished[:, moving], "inst", 0)
    finished = finished.at[:, moving].set(handed)
    return (finished[None, None], arrived[None, None])


def solution(mesh):
    in_specs = (
        P(("groups", "inst"), None, None, None),
        P(("groups", "inst"), "section", None, None, None, None, None),
        P(("groups", "inst"), None, None),
        P(("groups", "inst"), None),
        P(("groups", "inst"), None),
        P("section", None),
        P("section", None),
    )
    out_specs = (
        P(("groups", "inst"), "section", None, None, None),
        P(("groups", "inst"), "section", None, None, None, None, None, None),
    )
    return jax.shard_map(
        per_device, mesh=mesh, in_specs=in_specs, out_specs=out_specs, check_vma=False
    )
```

```python
import math

import jax
import jax.numpy as jnp
from jax import lax
from jax.sharding import PartitionSpec as P
from jax.experimental import pallas as pl
from jax.experimental.pallas import tpu as pltpu

CHUNKS = 4


def partner(block, axis, stride):
    count = lax.axis_size(axis)
    route = []
    for low in range(count):
        high = low | 1 << stride
        if high != low and high < count:
            route += [(low, high), (high, low)]
    return lax.ppermute(block, axis, route)


def passed_along(array, axis, by):
    peers = lax.axis_size(axis)
    pairs = [(i, i + by) for i in range(peers) if 0 <= i + by < peers]
    return lax.ppermute(array, axis, pairs)


def layer(rows, keys, values, lens, gain, scale):
    steps, reqs, width = rows.shape
    pages = keys.shape[1]
    kv_heads = keys.shape[2]
    page_len = keys.shape[3]
    head = keys.shape[4]
    group = width // (kv_heads * head)
    wide = rows.astype(jnp.float32)
    normed = wide * lax.rsqrt(jnp.mean(wide * wide, axis=-1, keepdims=True) + 1e-05) * gain
    heads = normed.reshape(steps, reqs, kv_heads, group, head)
    query = jnp.transpose(heads.astype(jnp.bfloat16), (1, 2, 0, 3, 4))
    query = query.reshape(reqs, kv_heads, steps * group, head)
    fresh = jnp.mean(heads, axis=3).astype(jnp.bfloat16)
    fresh = jnp.transpose(fresh, (1, 2, 0, 3))
    factor = 1.0 / math.sqrt(head)
    wide_query = jnp.broadcast_to(query[:, None], (reqs, pages) + query.shape[1:])
    cache_scores = (
        jnp.einsum("rjgxd,rjgpd->rjgxp", wide_query, keys, preferred_element_type=jnp.float32)
        * factor
    )
    positions = jnp.arange(pages)[:, None] * page_len + jnp.arange(page_len)[None, :]
    live = positions[None] < lens[:, None, None]
    cache_scores = jnp.where(live[:, :, None, None, :], cache_scores, -1e30)
    new_scores = (
        jnp.einsum("rgxd,rgsd->rgxs", query, fresh, preferred_element_type=jnp.float32) * factor
    )
    step_of = jnp.arange(steps * group) // group
    done = jnp.arange(steps)[None, :] <= step_of[:, None]
    new_scores = jnp.where(done[None, None], new_scores, -1e30)
    top = jnp.maximum(
        jnp.max(cache_scores, axis=(1, 4)), jnp.max(new_scores, axis=-1)
    )[..., None]
    cache_exp = jnp.exp(cache_scores - top[:, None])
    new_exp = jnp.exp(new_scores - top)
    total = jnp.sum(cache_exp, axis=(1, 4))[..., None] + jnp.sum(new_exp, axis=-1, keepdims=True)
    cache_w = (cache_exp / total[:, None]).astype(jnp.bfloat16)
    new_w = (new_exp / total).astype(jnp.bfloat16)
    attended = jnp.einsum(
        "rjgxp,rjgpd->rjgxd", cache_w, values, preferred_element_type=jnp.float32
    ).sum(axis=1)
    attended = attended + jnp.einsum(
        "rgxs,rgsd->rgxd", new_w, fresh, preferred_element_type=jnp.float32
    )
    attended = attended.reshape(reqs, kv_heads, steps, group, head)
    attended = jnp.transpose(attended, (2, 0, 1, 3, 4)).reshape(steps, reqs, width)
    return (wide + scale * attended).astype(jnp.bfloat16)


def copy_kernel(table_ref, page_ref, *refs):
    keys_ref, values_ref = refs[-2], refs[-1]
    keys_ref[0, 0] = page_ref[0, 0]
    values_ref[0, 0] = page_ref[0, 1]


def gather_chunk(pool, table, chunk, block, previous):
    reqs, pages = table.shape
    kv_heads, page_len, head = pool.shape[2:]

    def page_index(r, j, table_ref):
        return (table_ref[(chunk * block + r) * pages + j], 0, 0, 0, 0)

    def slot_index(r, j, table_ref):
        return (chunk * block + r, j, 0, 0, 0)

    slot = pl.BlockSpec((1, 1, kv_heads, page_len, head), slot_index)
    in_specs = [pl.BlockSpec((1, 2, kv_heads, page_len, head), page_index)]
    operands = [table.reshape(-1), pool]
    aliases = {}
    if previous is not None:
        in_specs += [pl.BlockSpec(memory_space=pl.ANY)] * 2
        operands += list(previous)
        aliases = {2: 0, 3: 1}
    grid_spec = pltpu.PrefetchScalarGridSpec(
        num_scalar_prefetch=1,
        grid=(block, pages),
        in_specs=in_specs,
        out_specs=[slot, slot],
    )
    half = jax.ShapeDtypeStruct((reqs, pages, kv_heads, page_len, head), pool.dtype)
    return pl.pallas_call(
        copy_kernel, grid_spec=grid_spec, out_shape=[half, half], input_output_aliases=aliases
    )(*operands)

def per_device(tokens, kv_pool, page_table, lengths, migrate_ids, norm_gain, out_scale):
    inputs = tokens[0]
    pool = kv_pool[0, 0]
    table = page_table[0]
    lens = lengths[0]
    moving = migrate_ids[0]
    gain = norm_gain[0]
    scale = out_scale[0]
    steps, reqs, width = inputs.shape
    page_len = pool.shape[3]
    chosen = table[moving]
    spots = jnp.arange(chosen.shape[1])[:, None] * page_len + jnp.arange(page_len)[None, :]
    arrived_lens = partner(lens[moving], "inst", 0)
    lens_used = lens
    section = lax.axis_index("section")
    count = lax.axis_size("section")
    chunks = CHUNKS
    block = reqs // chunks

    incoming = jnp.zeros((steps, block, width), jnp.bfloat16)
    keys, values = None, None
    results = []
    for k in range(chunks + count - 1):
        if k < chunks:
            previous = None if keys is None else (keys, values)
            keys, values = gather_chunk(pool, table, k, block, previous)
        item = k - section
        start = jnp.clip(item, 0, chunks - 1) * block
        if k == 3:
            start, incoming, chosen = lax.optimization_barrier((start, incoming, chosen))
            received = partner(pool[chosen], "inst", 0)
            keep = spots[None, :, :] < arrived_lens[:, None, None]
            arrived = jnp.where(
                keep[:, :, None, None, :, None], received, jnp.zeros((), jnp.bfloat16)
            )
        elif k == 6:
            start, incoming, arrived = lax.optimization_barrier((start, incoming, arrived))
        elif k > 0:
            start, incoming = lax.optimization_barrier((start, incoming))
        first = lax.dynamic_slice_in_dim(inputs, start, block, 1)
        rows = jnp.where(section == 0, first, incoming)
        part_keys = lax.dynamic_slice_in_dim(keys, start, block, 0)
        part_values = lax.dynamic_slice_in_dim(values, start, block, 0)
        part_lens = lax.dynamic_slice_in_dim(lens_used, start, block, 0)
        result = layer(rows, part_keys, part_values, part_lens, gain, scale)
        results.append(result)
        pairs = [(s, s + 1) for s in range(count - 1) if 0 <= k - s < chunks]
        if pairs:
            incoming = lax.ppermute(result, "section", pairs)
    stacked = jnp.stack(results)
    finished = jnp.concatenate(
        [lax.dynamic_index_in_dim(stacked, c + section, 0, False) for c in range(chunks)], axis=1
    )
    handed = partner(finished[:, moving], "inst", 0)
    finished = finished.at[:, moving].set(handed)
    return (finished[None, None], arrived[None, None])


def solution(mesh):
    in_specs = (
        P(("groups", "inst"), None, None, None),
        P(("groups", "inst"), "section", None, None, None, None, None),
        P(("groups", "inst"), None, None),
        P(("groups", "inst"), None),
        P(("groups", "inst"), None),
        P("section", None),
        P("section", None),
    )
    out_specs = (
        P(("groups", "inst"), "section", None, None, None),
        P(("groups", "inst"), "section", None, None, None, None, None, None),
    )
    return jax.shard_map(
        per_device, mesh=mesh, in_specs=in_specs, out_specs=out_specs, check_vma=False
    )
```

```python
import math

import jax
import jax.numpy as jnp
from jax import lax
from jax.sharding import PartitionSpec as P
from jax.experimental import pallas as pl
from jax.experimental.pallas import tpu as pltpu

CHUNKS = 4


def partner(block, axis, stride):
    count = lax.axis_size(axis)
    route = []
    for low in range(count):
        high = low | 1 << stride
        if high != low and high < count:
            route += [(low, high), (high, low)]
    return lax.ppermute(block, axis, route)


def passed_along(array, axis, by):
    peers = lax.axis_size(axis)
    pairs = [(i, i + by) for i in range(peers) if 0 <= i + by < peers]
    return lax.ppermute(array, axis, pairs)


def layer(rows, keys, values, lens, gain, scale):
    steps, reqs, width = rows.shape
    pages = keys.shape[1]
    kv_heads = keys.shape[2]
    page_len = keys.shape[3]
    head = keys.shape[4]
    group = width // (kv_heads * head)
    wide = rows.astype(jnp.float32)
    normed = wide * lax.rsqrt(jnp.mean(wide * wide, axis=-1, keepdims=True) + 1e-05) * gain
    heads = normed.reshape(steps, reqs, kv_heads, group, head)
    query = jnp.transpose(heads.astype(jnp.bfloat16), (1, 2, 0, 3, 4))
    query = query.reshape(reqs, kv_heads, steps * group, head)
    fresh = jnp.mean(heads, axis=3).astype(jnp.bfloat16)
    fresh = jnp.transpose(fresh, (1, 2, 0, 3))
    factor = 1.0 / math.sqrt(head)
    wide_query = jnp.broadcast_to(query[:, None], (reqs, pages) + query.shape[1:])
    cache_scores = (
        jnp.einsum("rjgxd,rjgpd->rjgxp", wide_query, keys, preferred_element_type=jnp.float32)
        * factor
    )
    positions = jnp.arange(pages)[:, None] * page_len + jnp.arange(page_len)[None, :]
    live = positions[None] < lens[:, None, None]
    cache_scores = jnp.where(live[:, :, None, None, :], cache_scores, -1e30)
    new_scores = (
        jnp.einsum("rgxd,rgsd->rgxs", query, fresh, preferred_element_type=jnp.float32) * factor
    )
    step_of = jnp.arange(steps * group) // group
    done = jnp.arange(steps)[None, :] <= step_of[:, None]
    new_scores = jnp.where(done[None, None], new_scores, -1e30)
    top = jnp.maximum(
        jnp.max(cache_scores, axis=(1, 4)), jnp.max(new_scores, axis=-1)
    )[..., None]
    cache_exp = jnp.exp(cache_scores - top[:, None])
    new_exp = jnp.exp(new_scores - top)
    total = jnp.sum(cache_exp, axis=(1, 4))[..., None] + jnp.sum(new_exp, axis=-1, keepdims=True)
    cache_w = (cache_exp / total[:, None]).astype(jnp.bfloat16)
    new_w = (new_exp / total).astype(jnp.bfloat16)
    attended = jnp.einsum(
        "rjgxp,rjgpd->rjgxd", cache_w, values, preferred_element_type=jnp.float32
    ).sum(axis=1)
    attended = attended + jnp.einsum(
        "rgxs,rgsd->rgxd", new_w, fresh, preferred_element_type=jnp.float32
    )
    attended = attended.reshape(reqs, kv_heads, steps, group, head)
    attended = jnp.transpose(attended, (2, 0, 1, 3, 4)).reshape(steps, reqs, width)
    return (wide + scale * attended).astype(jnp.bfloat16)


def copy_kernel(table_ref, page_ref, *refs):
    keys_ref, values_ref = refs[-2], refs[-1]
    keys_ref[0, 0] = page_ref[0, 0]
    values_ref[0, 0] = page_ref[0, 1]


def gather_chunk(pool, table, chunk, block, previous):
    reqs, pages = table.shape
    kv_heads, page_len, head = pool.shape[2:]

    def page_index(r, j, table_ref):
        return (table_ref[(chunk * block + r) * pages + j], 0, 0, 0, 0)

    def slot_index(r, j, table_ref):
        return (chunk * block + r, j, 0, 0, 0)

    slot = pl.BlockSpec((1, 1, kv_heads, page_len, head), slot_index)
    in_specs = [pl.BlockSpec((1, 2, kv_heads, page_len, head), page_index)]
    operands = [table.reshape(-1), pool]
    aliases = {}
    if previous is not None:
        in_specs += [pl.BlockSpec(memory_space=pl.ANY)] * 2
        operands += list(previous)
        aliases = {2: 0, 3: 1}
    grid_spec = pltpu.PrefetchScalarGridSpec(
        num_scalar_prefetch=1,
        grid=(block, pages),
        in_specs=in_specs,
        out_specs=[slot, slot],
    )
    half = jax.ShapeDtypeStruct((reqs, pages, kv_heads, page_len, head), pool.dtype)
    return pl.pallas_call(
        copy_kernel, grid_spec=grid_spec, out_shape=[half, half], input_output_aliases=aliases
    )(*operands)

def per_device(tokens, kv_pool, page_table, lengths, migrate_ids, norm_gain, out_scale):
    inputs = tokens[0]
    pool = kv_pool[0, 0]
    table = page_table[0]
    lens = lengths[0]
    moving = migrate_ids[0]
    gain = norm_gain[0]
    scale = out_scale[0]
    steps, reqs, width = inputs.shape
    page_len = pool.shape[3]
    chosen = table[moving]
    spots = jnp.arange(chosen.shape[1])[:, None] * page_len + jnp.arange(page_len)[None, :]
    arrived_lens = partner(lens[moving], "inst", 0)
    lens_used = lens
    section = lax.axis_index("section")
    count = lax.axis_size("section")
    chunks = CHUNKS
    block = reqs // chunks

    incoming = jnp.zeros((steps, block, width), jnp.bfloat16)
    keys, values = None, None
    results = []
    for k in range(chunks + count - 1):
        if k < chunks:
            previous = None if keys is None else (keys, values)
            keys, values = gather_chunk(pool, table, k, block, previous)
        item = k - section
        start = jnp.clip(item, 0, chunks - 1) * block
        if k == 3:
            start, incoming, chosen = lax.optimization_barrier((start, incoming, chosen))
            received = partner(pool[chosen], "inst", 0)
            keep = spots[None, :, :] < arrived_lens[:, None, None]
            arrived = jnp.where(
                keep[:, :, None, None, :, None], received, jnp.zeros((), jnp.bfloat16)
            )
        elif k == 6:
            start, incoming, arrived = lax.optimization_barrier((start, incoming, arrived))
        elif k > 0:
            start, incoming = lax.optimization_barrier((start, incoming))
        first = lax.dynamic_slice_in_dim(inputs, start, block, 1)
        rows = jnp.where(section == 0, first, incoming)
        part_keys = lax.dynamic_slice_in_dim(keys, start, block, 0)
        part_values = lax.dynamic_slice_in_dim(values, start, block, 0)
        part_lens = lax.dynamic_slice_in_dim(lens_used, start, block, 0)
        result = layer(rows, part_keys, part_values, part_lens, gain, scale)
        results.append(result)
        pairs = [(s, s + 1) for s in range(count - 1) if 0 <= k - s < chunks]
        if pairs:
            incoming = lax.ppermute(result, "section", pairs)
    stacked = jnp.stack(results)
    finished = jnp.concatenate(
        [lax.dynamic_index_in_dim(stacked, c + section, 0, False) for c in range(chunks)], axis=1
    )
    handed = partner(finished[:, moving], "inst", 0)
    hit = jnp.arange(reqs)[:, None] == moving[None, :]
    handed_full = jnp.take(handed, jnp.argmax(hit, axis=1), axis=1)
    finished = jnp.where(jnp.any(hit, axis=1)[None, :, None], handed_full, finished)
    return (finished[None, None], arrived[None, None])


def solution(mesh):
    in_specs = (
        P(("groups", "inst"), None, None, None),
        P(("groups", "inst"), "section", None, None, None, None, None),
        P(("groups", "inst"), None, None),
        P(("groups", "inst"), None),
        P(("groups", "inst"), None),
        P("section", None),
        P("section", None),
    )
    out_specs = (
        P(("groups", "inst"), "section", None, None, None),
        P(("groups", "inst"), "section", None, None, None, None, None, None),
    )
    return jax.shard_map(
        per_device, mesh=mesh, in_specs=in_specs, out_specs=out_specs, check_vma=False
    )
```

```python
import math

import jax
import jax.numpy as jnp
from jax import lax
from jax.sharding import PartitionSpec as P
from jax.experimental import pallas as pl
from jax.experimental.pallas import tpu as pltpu

CHUNKS = 4


def partner(block, axis, stride):
    count = lax.axis_size(axis)
    route = []
    for low in range(count):
        high = low | 1 << stride
        if high != low and high < count:
            route += [(low, high), (high, low)]
    return lax.ppermute(block, axis, route)


def passed_along(array, axis, by):
    peers = lax.axis_size(axis)
    pairs = [(i, i + by) for i in range(peers) if 0 <= i + by < peers]
    return lax.ppermute(array, axis, pairs)


def layer(rows, keys, values, lens, gain, scale):
    steps, reqs, width = rows.shape
    pages = keys.shape[1]
    kv_heads = keys.shape[2]
    page_len = keys.shape[3]
    head = keys.shape[4]
    group = width // (kv_heads * head)
    wide = rows.astype(jnp.float32)
    normed = wide * lax.rsqrt(jnp.mean(wide * wide, axis=-1, keepdims=True) + 1e-05) * gain
    heads = normed.reshape(steps, reqs, kv_heads, group, head)
    query = jnp.transpose(heads.astype(jnp.bfloat16), (1, 2, 0, 3, 4))
    query = query.reshape(reqs, kv_heads, steps * group, head)
    fresh = jnp.mean(heads, axis=3).astype(jnp.bfloat16)
    fresh = jnp.transpose(fresh, (1, 2, 0, 3))
    factor = 1.0 / math.sqrt(head)
    wide_query = jnp.broadcast_to(query[:, None], (reqs, pages) + query.shape[1:])
    cache_scores = (
        jnp.einsum("rjgxd,rjgpd->rjgxp", wide_query, keys, preferred_element_type=jnp.float32)
        * factor
    )
    positions = jnp.arange(pages)[:, None] * page_len + jnp.arange(page_len)[None, :]
    live = positions[None] < lens[:, None, None]
    cache_scores = jnp.where(live[:, :, None, None, :], cache_scores, -1e30)
    new_scores = (
        jnp.einsum("rgxd,rgsd->rgxs", query, fresh, preferred_element_type=jnp.float32) * factor
    )
    step_of = jnp.arange(steps * group) // group
    done = jnp.arange(steps)[None, :] <= step_of[:, None]
    new_scores = jnp.where(done[None, None], new_scores, -1e30)
    top = jnp.maximum(
        jnp.max(cache_scores, axis=(1, 4)), jnp.max(new_scores, axis=-1)
    )[..., None]
    cache_exp = jnp.exp(cache_scores - top[:, None])
    new_exp = jnp.exp(new_scores - top)
    total = jnp.sum(cache_exp, axis=(1, 4))[..., None] + jnp.sum(new_exp, axis=-1, keepdims=True)
    cache_w = (cache_exp / total[:, None]).astype(jnp.bfloat16)
    new_w = (new_exp / total).astype(jnp.bfloat16)
    attended = jnp.einsum(
        "rjgxp,rjgpd->rjgxd", cache_w, values, preferred_element_type=jnp.float32
    ).sum(axis=1)
    attended = attended + jnp.einsum(
        "rgxs,rgsd->rgxd", new_w, fresh, preferred_element_type=jnp.float32
    )
    attended = attended.reshape(reqs, kv_heads, steps, group, head)
    attended = jnp.transpose(attended, (2, 0, 1, 3, 4)).reshape(steps, reqs, width)
    return (wide + scale * attended).astype(jnp.bfloat16)


def copy_kernel(table_ref, page_ref, *refs):
    keys_ref, values_ref = refs[-2], refs[-1]
    keys_ref[0, 0] = page_ref[0, 0]
    values_ref[0, 0] = page_ref[0, 1]


def gather_chunk(pool, table, chunk, block, previous):
    reqs, pages = table.shape
    kv_heads, page_len, head = pool.shape[2:]

    def page_index(r, j, table_ref):
        return (table_ref[chunk * block + r, j], 0, 0, 0, 0)

    def slot_index(r, j, table_ref):
        return (chunk * block + r, j, 0, 0, 0)

    slot = pl.BlockSpec((1, 1, kv_heads, page_len, head), slot_index)
    in_specs = [pl.BlockSpec((1, 2, kv_heads, page_len, head), page_index)]
    operands = [table, pool]
    aliases = {}
    if previous is not None:
        in_specs += [pl.BlockSpec(memory_space=pl.ANY)] * 2
        operands += list(previous)
        aliases = {2: 0, 3: 1}
    grid_spec = pltpu.PrefetchScalarGridSpec(
        num_scalar_prefetch=1,
        grid=(block, pages),
        in_specs=in_specs,
        out_specs=[slot, slot],
    )
    half = jax.ShapeDtypeStruct((reqs, pages, kv_heads, page_len, head), pool.dtype)
    return pl.pallas_call(
        copy_kernel, grid_spec=grid_spec, out_shape=[half, half], input_output_aliases=aliases
    )(*operands)

def per_device(tokens, kv_pool, page_table, lengths, migrate_ids, norm_gain, out_scale):
    inputs = tokens[0]
    pool = kv_pool[0, 0]
    table = page_table[0]
    lens = lengths[0]
    moving = migrate_ids[0]
    gain = norm_gain[0]
    scale = out_scale[0]
    steps, reqs, width = inputs.shape
    page_len = pool.shape[3]
    chosen = table[moving]
    spots = jnp.arange(chosen.shape[1])[:, None] * page_len + jnp.arange(page_len)[None, :]
    arrived_lens = partner(lens[moving], "inst", 0)
    lens_used = lens
    section = lax.axis_index("section")
    count = lax.axis_size("section")
    chunks = CHUNKS
    block = reqs // chunks

    incoming = jnp.zeros((steps, block, width), jnp.bfloat16)
    keys, values = None, None
    results = []
    for k in range(chunks + count - 1):
        if k < chunks:
            previous = None if keys is None else (keys, values)
            keys, values = gather_chunk(pool, table, k, block, previous)
        item = k - section
        start = jnp.clip(item, 0, chunks - 1) * block
        if k == 3:
            start, incoming, chosen = lax.optimization_barrier((start, incoming, chosen))
            received = partner(pool[chosen], "inst", 0)
            keep = spots[None, :, :] < arrived_lens[:, None, None]
            arrived = jnp.where(
                keep[:, :, None, None, :, None], received, jnp.zeros((), jnp.bfloat16)
            )
        elif k == 6:
            start, incoming, arrived = lax.optimization_barrier((start, incoming, arrived))
        elif k > 0:
            start, incoming = lax.optimization_barrier((start, incoming))
        first = lax.dynamic_slice_in_dim(inputs, start, block, 1)
        rows = jnp.where(section == 0, first, incoming)
        part_keys = lax.dynamic_slice_in_dim(keys, start, block, 0)
        part_values = lax.dynamic_slice_in_dim(values, start, block, 0)
        part_lens = lax.dynamic_slice_in_dim(lens_used, start, block, 0)
        result = layer(rows, part_keys, part_values, part_lens, gain, scale)
        results.append(result)
        pairs = [(s, s + 1) for s in range(count - 1) if 0 <= k - s < chunks]
        if pairs:
            incoming = lax.ppermute(result, "section", pairs)
    stacked = jnp.stack(results)
    finished = jnp.concatenate(
        [lax.dynamic_index_in_dim(stacked, c + section, 0, False) for c in range(chunks)], axis=1
    )
    handed = partner(finished[:, moving], "inst", 0)
    finished = finished.at[:, moving].set(handed)
    return (finished[None, None], arrived[None, None])


def solution(mesh):
    in_specs = (
        P(("groups", "inst"), None, None, None),
        P(("groups", "inst"), "section", None, None, None, None, None),
        P(("groups", "inst"), None, None),
        P(("groups", "inst"), None),
        P(("groups", "inst"), None),
        P("section", None),
        P("section", None),
    )
    out_specs = (
        P(("groups", "inst"), "section", None, None, None),
        P(("groups", "inst"), "section", None, None, None, None, None, None),
    )
    return jax.shard_map(
        per_device, mesh=mesh, in_specs=in_specs, out_specs=out_specs, check_vma=False
    )
```

```python
import math

import jax
import jax.numpy as jnp
from jax import lax
from jax.sharding import PartitionSpec as P
from jax.experimental import pallas as pl
from jax.experimental.pallas import tpu as pltpu

CHUNKS = 4


def partner(block, axis, stride):
    count = lax.axis_size(axis)
    route = []
    for low in range(count):
        high = low | 1 << stride
        if high != low and high < count:
            route += [(low, high), (high, low)]
    return lax.ppermute(block, axis, route)


def passed_along(array, axis, by):
    peers = lax.axis_size(axis)
    pairs = [(i, i + by) for i in range(peers) if 0 <= i + by < peers]
    return lax.ppermute(array, axis, pairs)


def layer(rows, keys, values, lens, gain, scale):
    steps, reqs, width = rows.shape
    pages = keys.shape[1]
    kv_heads = keys.shape[2]
    page_len = keys.shape[3]
    head = keys.shape[4]
    group = width // (kv_heads * head)
    wide = rows.astype(jnp.float32)
    normed = wide * lax.rsqrt(jnp.mean(wide * wide, axis=-1, keepdims=True) + 1e-05) * gain
    heads = normed.reshape(steps, reqs, kv_heads, group, head)
    query = jnp.transpose(heads.astype(jnp.bfloat16), (1, 2, 0, 3, 4))
    query = query.reshape(reqs, kv_heads, steps * group, head)
    fresh = jnp.mean(heads, axis=3).astype(jnp.bfloat16)
    fresh = jnp.transpose(fresh, (1, 2, 0, 3))
    factor = 1.0 / math.sqrt(head)
    wide_query = jnp.broadcast_to(query[:, None], (reqs, pages) + query.shape[1:])
    cache_scores = (
        jnp.einsum("rjgxd,rjgpd->rjgxp", wide_query, keys, preferred_element_type=jnp.float32)
        * factor
    )
    positions = jnp.arange(pages)[:, None] * page_len + jnp.arange(page_len)[None, :]
    live = positions[None] < lens[:, None, None]
    cache_scores = jnp.where(live[:, :, None, None, :], cache_scores, -1e30)
    new_scores = (
        jnp.einsum("rgxd,rgsd->rgxs", query, fresh, preferred_element_type=jnp.float32) * factor
    )
    step_of = jnp.arange(steps * group) // group
    done = jnp.arange(steps)[None, :] <= step_of[:, None]
    new_scores = jnp.where(done[None, None], new_scores, -1e30)
    top = jnp.maximum(
        jnp.max(cache_scores, axis=(1, 4)), jnp.max(new_scores, axis=-1)
    )[..., None]
    cache_exp = jnp.exp(cache_scores - top[:, None])
    new_exp = jnp.exp(new_scores - top)
    total = jnp.sum(cache_exp, axis=(1, 4))[..., None] + jnp.sum(new_exp, axis=-1, keepdims=True)
    cache_w = (cache_exp / total[:, None]).astype(jnp.bfloat16)
    new_w = (new_exp / total).astype(jnp.bfloat16)
    attended = jnp.einsum(
        "rjgxp,rjgpd->rjgxd", cache_w, values, preferred_element_type=jnp.float32
    ).sum(axis=1)
    attended = attended + jnp.einsum(
        "rgxs,rgsd->rgxd", new_w, fresh, preferred_element_type=jnp.float32
    )
    attended = attended.reshape(reqs, kv_heads, steps, group, head)
    attended = jnp.transpose(attended, (2, 0, 1, 3, 4)).reshape(steps, reqs, width)
    return (wide + scale * attended).astype(jnp.bfloat16)


def copy_kernel(table_ref, page_ref, *refs):
    keys_ref, values_ref = refs[-2], refs[-1]
    keys_ref[0, 0] = page_ref[0, 0]
    values_ref[0, 0] = page_ref[0, 1]


def gather_chunk(pool, table, chunk, block, previous):
    reqs, pages = table.shape
    kv_heads, page_len, head = pool.shape[2:]

    def page_index(r, j, table_ref):
        return (table_ref[(chunk * block + r) * pages + j], 0, 0, 0, 0)

    def slot_index(r, j, table_ref):
        return (chunk * block + r, j, 0, 0, 0)

    slot = pl.BlockSpec((1, 1, kv_heads, page_len, head), slot_index)
    in_specs = [pl.BlockSpec((1, 2, kv_heads, page_len, head), page_index)]
    operands = [table.reshape(-1), pool]
    aliases = {}
    if previous is not None:
        in_specs += [pl.BlockSpec(memory_space=pl.ANY)] * 2
        operands += list(previous)
        aliases = {2: 0, 3: 1}
    grid_spec = pltpu.PrefetchScalarGridSpec(
        num_scalar_prefetch=1,
        grid=(block, pages),
        in_specs=in_specs,
        out_specs=[slot, slot],
    )
    half = jax.ShapeDtypeStruct((reqs, pages, kv_heads, page_len, head), pool.dtype)
    return pl.pallas_call(
        copy_kernel, grid_spec=grid_spec, out_shape=[half, half], input_output_aliases=aliases
    )(*operands)

def per_device(tokens, kv_pool, page_table, lengths, migrate_ids, norm_gain, out_scale):
    inputs = tokens[0]
    pool = kv_pool[0, 0]
    table = page_table[0]
    lens = lengths[0]
    moving = migrate_ids[0]
    gain = norm_gain[0]
    scale = out_scale[0]
    steps, reqs, width = inputs.shape
    page_len = pool.shape[3]
    chosen = table[moving]
    spots = jnp.arange(chosen.shape[1])[:, None] * page_len + jnp.arange(page_len)[None, :]
    arrived_lens = partner(lens[moving], "inst", 0)
    lens_used = lens
    section = lax.axis_index("section")
    count = lax.axis_size("section")
    chunks = CHUNKS
    block = reqs // chunks

    incoming = jnp.zeros((steps, block, width), jnp.bfloat16)
    keys, values = None, None
    results = []
    for k in range(chunks + count - 1):
        if k < chunks:
            previous = None if keys is None else (keys, values)
            keys, values = gather_chunk(pool, table, k, block, previous)
        item = k - section
        start = jnp.clip(item, 0, chunks - 1) * block
        if k == 3:
            start, incoming, chosen = lax.optimization_barrier((start, incoming, chosen))
            received = partner(pool[chosen], "inst", 0)
            keep = spots[None, :, :] < arrived_lens[:, None, None]
            arrived = jnp.where(
                keep[:, :, None, None, :, None], received, jnp.zeros((), jnp.bfloat16)
            )
        elif k == 6:
            start, incoming, arrived = lax.optimization_barrier((start, incoming, arrived))
        elif k > 0:
            start, incoming = lax.optimization_barrier((start, incoming))
        if k == 0:
            rows = inputs[:, :block]
        elif k < chunks:
            first = lax.dynamic_slice_in_dim(inputs, start, block, 1)
            rows = jnp.where(section == 0, first, incoming)
        else:
            rows = incoming
        part_keys = lax.dynamic_slice_in_dim(keys, start, block, 0)
        part_values = lax.dynamic_slice_in_dim(values, start, block, 0)
        part_lens = lax.dynamic_slice_in_dim(lens_used, start, block, 0)
        result = layer(rows, part_keys, part_values, part_lens, gain, scale)
        results.append(result)
        pairs = [(s, s + 1) for s in range(count - 1) if 0 <= k - s < chunks]
        if pairs:
            incoming = lax.ppermute(result, "section", pairs)
    stacked = jnp.stack(results)
    finished = jnp.concatenate(
        [lax.dynamic_index_in_dim(stacked, c + section, 0, False) for c in range(chunks)], axis=1
    )
    handed = partner(finished[:, moving], "inst", 0)
    finished = finished.at[:, moving].set(handed)
    return (finished[None, None], arrived[None, None])


def solution(mesh):
    in_specs = (
        P(("groups", "inst"), None, None, None),
        P(("groups", "inst"), "section", None, None, None, None, None),
        P(("groups", "inst"), None, None),
        P(("groups", "inst"), None),
        P(("groups", "inst"), None),
        P("section", None),
        P("section", None),
    )
    out_specs = (
        P(("groups", "inst"), "section", None, None, None),
        P(("groups", "inst"), "section", None, None, None, None, None, None),
    )
    return jax.shard_map(
        per_device, mesh=mesh, in_specs=in_specs, out_specs=out_specs, check_vma=False
    )
```

```python
import math

import jax
import jax.numpy as jnp
from jax import lax
from jax.sharding import PartitionSpec as P
from jax.experimental import pallas as pl
from jax.experimental.pallas import tpu as pltpu

CHUNKS = 4


def partner(block, axis, stride):
    count = lax.axis_size(axis)
    route = []
    for low in range(count):
        high = low | 1 << stride
        if high != low and high < count:
            route += [(low, high), (high, low)]
    return lax.ppermute(block, axis, route)


def passed_along(array, axis, by):
    peers = lax.axis_size(axis)
    pairs = [(i, i + by) for i in range(peers) if 0 <= i + by < peers]
    return lax.ppermute(array, axis, pairs)


def layer(rows, keys, values, lens, gain, scale):
    steps, reqs, width = rows.shape
    pages = keys.shape[1]
    kv_heads = keys.shape[2]
    page_len = keys.shape[3]
    head = keys.shape[4]
    group = width // (kv_heads * head)
    wide = rows.astype(jnp.float32)
    normed = wide * lax.rsqrt(jnp.mean(wide * wide, axis=-1, keepdims=True) + 1e-05) * gain
    heads = normed.reshape(steps, reqs, kv_heads, group, head)
    query = jnp.transpose(heads.astype(jnp.bfloat16), (1, 2, 0, 3, 4))
    query = query.reshape(reqs, kv_heads, steps * group, head)
    fresh = jnp.mean(heads, axis=3).astype(jnp.bfloat16)
    fresh = jnp.transpose(fresh, (1, 2, 0, 3))
    factor = 1.0 / math.sqrt(head)
    wide_query = jnp.broadcast_to(query[:, None], (reqs, pages) + query.shape[1:])
    cache_scores = (
        jnp.einsum("rjgxd,rjgpd->rjgxp", wide_query, keys, preferred_element_type=jnp.float32)
        * factor
    )
    positions = jnp.arange(pages)[:, None] * page_len + jnp.arange(page_len)[None, :]
    live = positions[None] < lens[:, None, None]
    cache_scores = jnp.where(live[:, :, None, None, :], cache_scores, -1e30)
    new_scores = (
        jnp.einsum("rgxd,rgsd->rgxs", query, fresh, preferred_element_type=jnp.float32) * factor
    )
    step_of = jnp.arange(steps * group) // group
    done = jnp.arange(steps)[None, :] <= step_of[:, None]
    new_scores = jnp.where(done[None, None], new_scores, -1e30)
    top = jnp.maximum(
        jnp.max(cache_scores, axis=(1, 4)), jnp.max(new_scores, axis=-1)
    )[..., None]
    cache_exp = jnp.exp(cache_scores - top[:, None])
    new_exp = jnp.exp(new_scores - top)
    total = jnp.sum(cache_exp, axis=(1, 4))[..., None] + jnp.sum(new_exp, axis=-1, keepdims=True)
    cache_w = (cache_exp / total[:, None]).astype(jnp.bfloat16)
    new_w = (new_exp / total).astype(jnp.bfloat16)
    attended = jnp.einsum(
        "rjgxp,rjgpd->rjgxd", cache_w, values, preferred_element_type=jnp.float32
    ).sum(axis=1)
    attended = attended + jnp.einsum(
        "rgxs,rgsd->rgxd", new_w, fresh, preferred_element_type=jnp.float32
    )
    attended = attended.reshape(reqs, kv_heads, steps, group, head)
    attended = jnp.transpose(attended, (2, 0, 1, 3, 4)).reshape(steps, reqs, width)
    return (wide + scale * attended).astype(jnp.bfloat16)


def copy_kernel(table_ref, page_ref, *refs):
    keys_ref, values_ref = refs[-2], refs[-1]
    keys_ref[0, 0] = page_ref[0, 0]
    values_ref[0, 0] = page_ref[0, 1]


def gather_chunk(pool, table, chunk, block, previous):
    reqs, pages = table.shape
    kv_heads, page_len, head = pool.shape[2:]

    def page_index(r, j, table_ref):
        return (table_ref[(chunk * block + r) * pages + j], 0, 0, 0, 0)

    def slot_index(r, j, table_ref):
        return (chunk * block + r, j, 0, 0, 0)

    slot = pl.BlockSpec((1, 1, kv_heads, page_len, head), slot_index)
    in_specs = [pl.BlockSpec((1, 2, kv_heads, page_len, head), page_index)]
    operands = [table.reshape(-1), pool]
    aliases = {}
    if previous is not None:
        in_specs += [pl.BlockSpec(memory_space=pl.ANY)] * 2
        operands += list(previous)
        aliases = {2: 0, 3: 1}
    grid_spec = pltpu.PrefetchScalarGridSpec(
        num_scalar_prefetch=1,
        grid=(block, pages),
        in_specs=in_specs,
        out_specs=[slot, slot],
    )
    half = jax.ShapeDtypeStruct((reqs, pages, kv_heads, page_len, head), pool.dtype)
    return pl.pallas_call(
        copy_kernel, grid_spec=grid_spec, out_shape=[half, half], input_output_aliases=aliases
    )(*operands)

def per_device(tokens, kv_pool, page_table, lengths, migrate_ids, norm_gain, out_scale):
    inputs = tokens[0]
    pool = kv_pool[0, 0]
    table = page_table[0]
    lens = lengths[0]
    moving = migrate_ids[0]
    gain = norm_gain[0]
    scale = out_scale[0]
    steps, reqs, width = inputs.shape
    page_len = pool.shape[3]
    chosen = table[moving]
    spots = jnp.arange(chosen.shape[1])[:, None] * page_len + jnp.arange(page_len)[None, :]
    arrived_lens = partner(lens[moving], "inst", 0)
    lens_used = lens
    section = lax.axis_index("section")
    count = lax.axis_size("section")
    chunks = CHUNKS
    block = reqs // chunks

    incoming = jnp.zeros((steps, block, width), jnp.bfloat16)
    keys, values = None, None
    results = []
    for k in range(chunks + count - 1):
        if k < chunks:
            previous = None if keys is None else (keys, values)
            keys, values = gather_chunk(pool, table, k, block, previous)
        item = k - section
        start = jnp.clip(item, 0, chunks - 1) * block
        if k == 3:
            start, incoming, chosen = lax.optimization_barrier((start, incoming, chosen))
            received = partner(pool[chosen], "inst", 0)
            keep = spots[None, :, :] < arrived_lens[:, None, None]
            arrived = jnp.where(
                keep[:, :, None, None, :, None], received, jnp.zeros((), jnp.bfloat16)
            )
        elif k == 6:
            start, incoming, arrived = lax.optimization_barrier((start, incoming, arrived))
        elif k > 0:
            start, incoming = lax.optimization_barrier((start, incoming))
        if k == 0:
            rows = inputs[:, :block]
        elif k < chunks:
            first = lax.dynamic_slice_in_dim(inputs, start, block, 1)
            rows = jnp.where(section == 0, first, incoming)
        else:
            rows = incoming
        if k == 0:
            start = 0
        elif k == chunks + count - 2:
            start = (chunks - 1) * block
        part_keys = lax.dynamic_slice_in_dim(keys, start, block, 0)
        part_values = lax.dynamic_slice_in_dim(values, start, block, 0)
        part_lens = lax.dynamic_slice_in_dim(lens_used, start, block, 0)
        result = layer(rows, part_keys, part_values, part_lens, gain, scale)
        results.append(result)
        pairs = [(s, s + 1) for s in range(count - 1) if 0 <= k - s < chunks]
        if pairs:
            incoming = lax.ppermute(result, "section", pairs)
    stacked = jnp.stack(results)
    finished = jnp.concatenate(
        [lax.dynamic_index_in_dim(stacked, c + section, 0, False) for c in range(chunks)], axis=1
    )
    handed = partner(finished[:, moving], "inst", 0)
    finished = finished.at[:, moving].set(handed)
    return (finished[None, None], arrived[None, None])


def solution(mesh):
    in_specs = (
        P(("groups", "inst"), None, None, None),
        P(("groups", "inst"), "section", None, None, None, None, None),
        P(("groups", "inst"), None, None),
        P(("groups", "inst"), None),
        P(("groups", "inst"), None),
        P("section", None),
        P("section", None),
    )
    out_specs = (
        P(("groups", "inst"), "section", None, None, None),
        P(("groups", "inst"), "section", None, None, None, None, None, None),
    )
    return jax.shard_map(
        per_device, mesh=mesh, in_specs=in_specs, out_specs=out_specs, check_vma=False
    )
```

```python
import math

import jax
import jax.numpy as jnp
from jax import lax
from jax.sharding import PartitionSpec as P
from jax.experimental import pallas as pl
from jax.experimental.pallas import tpu as pltpu

CHUNKS = 4


def partner(block, axis, stride):
    count = lax.axis_size(axis)
    route = []
    for low in range(count):
        high = low | 1 << stride
        if high != low and high < count:
            route += [(low, high), (high, low)]
    return lax.ppermute(block, axis, route)


def passed_along(array, axis, by):
    peers = lax.axis_size(axis)
    pairs = [(i, i + by) for i in range(peers) if 0 <= i + by < peers]
    return lax.ppermute(array, axis, pairs)


def layer(rows, keys, values, lens, gain, scale):
    steps, reqs, width = rows.shape
    pages = keys.shape[1]
    kv_heads = keys.shape[2]
    page_len = keys.shape[3]
    head = keys.shape[4]
    group = width // (kv_heads * head)
    wide = rows.astype(jnp.float32)
    normed = wide * lax.rsqrt(jnp.mean(wide * wide, axis=-1, keepdims=True) + 1e-05) * gain
    heads = normed.reshape(steps, reqs, kv_heads, group, head)
    query = jnp.transpose(heads.astype(jnp.bfloat16), (1, 2, 0, 3, 4))
    query = query.reshape(reqs, kv_heads, steps * group, head)
    fresh = jnp.mean(heads, axis=3).astype(jnp.bfloat16)
    fresh = jnp.transpose(fresh, (1, 2, 0, 3))
    factor = 1.0 / math.sqrt(head)
    wide_query = jnp.broadcast_to(query[:, None], (reqs, pages) + query.shape[1:])
    cache_scores = (
        jnp.einsum("rjgxd,rjgpd->rjgxp", wide_query, keys, preferred_element_type=jnp.float32)
        * factor
    )
    positions = jnp.arange(pages)[:, None] * page_len + jnp.arange(page_len)[None, :]
    live = positions[None] < lens[:, None, None]
    cache_scores = jnp.where(live[:, :, None, None, :], cache_scores, -1e30)
    new_scores = (
        jnp.einsum("rgxd,rgsd->rgxs", query, fresh, preferred_element_type=jnp.float32) * factor
    )
    step_of = jnp.arange(steps * group) // group
    done = jnp.arange(steps)[None, :] <= step_of[:, None]
    new_scores = jnp.where(done[None, None], new_scores, -1e30)
    top = jnp.maximum(
        jnp.max(cache_scores, axis=(1, 4)), jnp.max(new_scores, axis=-1)
    )[..., None]
    cache_exp = jnp.exp(cache_scores - top[:, None])
    new_exp = jnp.exp(new_scores - top)
    total = jnp.sum(cache_exp, axis=(1, 4))[..., None] + jnp.sum(new_exp, axis=-1, keepdims=True)
    cache_w = (cache_exp / total[:, None]).astype(jnp.bfloat16)
    new_w = (new_exp / total).astype(jnp.bfloat16)
    attended = jnp.einsum(
        "rjgxp,rjgpd->rjgxd", cache_w, values, preferred_element_type=jnp.float32
    ).sum(axis=1)
    attended = attended + jnp.einsum(
        "rgxs,rgsd->rgxd", new_w, fresh, preferred_element_type=jnp.float32
    )
    attended = attended.reshape(reqs, kv_heads, steps, group, head)
    attended = jnp.transpose(attended, (2, 0, 1, 3, 4)).reshape(steps, reqs, width)
    return (wide + scale * attended).astype(jnp.bfloat16)


def copy_kernel(table_ref, page_ref, *refs):
    keys_ref, values_ref = refs[-2], refs[-1]
    keys_ref[0, 0] = page_ref[0, 0]
    values_ref[0, 0] = page_ref[0, 1]


def gather_chunk(pool, table, chunk, block, previous):
    reqs, pages = table.shape
    kv_heads, page_len, head = pool.shape[2:]

    def page_index(r, j, table_ref):
        return (table_ref[(chunk * block + r) * pages + j], 0, 0, 0, 0)

    def slot_index(r, j, table_ref):
        return (chunk * block + r, j, 0, 0, 0)

    slot = pl.BlockSpec((1, 1, kv_heads, page_len, head), slot_index)
    in_specs = [pl.BlockSpec((1, 2, kv_heads, page_len, head), page_index)]
    operands = [table.reshape(-1), pool]
    aliases = {}
    if previous is not None:
        in_specs += [pl.BlockSpec(memory_space=pl.ANY)] * 2
        operands += list(previous)
        aliases = {2: 0, 3: 1}
    grid_spec = pltpu.PrefetchScalarGridSpec(
        num_scalar_prefetch=1,
        grid=(block, pages),
        in_specs=in_specs,
        out_specs=[slot, slot],
    )
    half = jax.ShapeDtypeStruct((reqs, pages, kv_heads, page_len, head), pool.dtype)
    return pl.pallas_call(
        copy_kernel, grid_spec=grid_spec, out_shape=[half, half], input_output_aliases=aliases
    )(*operands)

def per_device(tokens, kv_pool, page_table, lengths, migrate_ids, norm_gain, out_scale):
    inputs = tokens[0]
    pool = kv_pool[0, 0]
    table = page_table[0]
    lens = lengths[0]
    moving = migrate_ids[0]
    gain = norm_gain[0]
    scale = out_scale[0]
    steps, reqs, width = inputs.shape
    page_len = pool.shape[3]
    chosen = table[moving]
    spots = jnp.arange(chosen.shape[1])[:, None] * page_len + jnp.arange(page_len)[None, :]
    arrived_lens = partner(lens[moving], "inst", 0)
    lens_used = lens
    section = lax.axis_index("section")
    count = lax.axis_size("section")
    chunks = CHUNKS
    block = reqs // chunks

    incoming = jnp.zeros((steps, block, width), jnp.bfloat16)
    keys, values = None, None
    results = []
    for k in range(chunks + count - 1):
        if k < chunks:
            previous = None if keys is None else (keys, values)
            keys, values = gather_chunk(pool, table, k, block, previous)
        item = k - section
        start = jnp.clip(item, 0, chunks - 1) * block
        if k == 1:
            start, incoming, chosen = lax.optimization_barrier((start, incoming, chosen))
            received = partner(pool[chosen], "inst", 0)
            keep = spots[None, :, :] < arrived_lens[:, None, None]
            arrived = jnp.where(
                keep[:, :, None, None, :, None], received, jnp.zeros((), jnp.bfloat16)
            )
        elif k == 4:
            start, incoming, arrived = lax.optimization_barrier((start, incoming, arrived))
        elif k > 0:
            start, incoming = lax.optimization_barrier((start, incoming))
        if k == 0:
            rows = inputs[:, :block]
        elif k < chunks:
            first = lax.dynamic_slice_in_dim(inputs, start, block, 1)
            rows = jnp.where(section == 0, first, incoming)
        else:
            rows = incoming
        part_keys = lax.dynamic_slice_in_dim(keys, start, block, 0)
        part_values = lax.dynamic_slice_in_dim(values, start, block, 0)
        part_lens = lax.dynamic_slice_in_dim(lens_used, start, block, 0)
        result = layer(rows, part_keys, part_values, part_lens, gain, scale)
        results.append(result)
        pairs = [(s, s + 1) for s in range(count - 1) if 0 <= k - s < chunks]
        if pairs:
            incoming = lax.ppermute(result, "section", pairs)
    stacked = jnp.stack(results)
    finished = jnp.concatenate(
        [lax.dynamic_index_in_dim(stacked, c + section, 0, False) for c in range(chunks)], axis=1
    )
    handed = partner(finished[:, moving], "inst", 0)
    finished = finished.at[:, moving].set(handed)
    return (finished[None, None], arrived[None, None])


def solution(mesh):
    in_specs = (
        P(("groups", "inst"), None, None, None),
        P(("groups", "inst"), "section", None, None, None, None, None),
        P(("groups", "inst"), None, None),
        P(("groups", "inst"), None),
        P(("groups", "inst"), None),
        P("section", None),
        P("section", None),
    )
    out_specs = (
        P(("groups", "inst"), "section", None, None, None),
        P(("groups", "inst"), "section", None, None, None, None, None, None),
    )
    return jax.shard_map(
        per_device, mesh=mesh, in_specs=in_specs, out_specs=out_specs, check_vma=False
    )
```

```python
import math

import jax
import jax.numpy as jnp
from jax import lax
from jax.sharding import PartitionSpec as P
from jax.experimental import pallas as pl
from jax.experimental.pallas import tpu as pltpu

CHUNKS = 4


def partner(block, axis, stride):
    count = lax.axis_size(axis)
    route = []
    for low in range(count):
        high = low | 1 << stride
        if high != low and high < count:
            route += [(low, high), (high, low)]
    return lax.ppermute(block, axis, route)


def passed_along(array, axis, by):
    peers = lax.axis_size(axis)
    pairs = [(i, i + by) for i in range(peers) if 0 <= i + by < peers]
    return lax.ppermute(array, axis, pairs)


def layer(rows, keys, values, lens, gain, scale):
    steps, reqs, width = rows.shape
    pages = keys.shape[1]
    kv_heads = keys.shape[2]
    page_len = keys.shape[3]
    head = keys.shape[4]
    group = width // (kv_heads * head)
    wide = rows.astype(jnp.float32)
    normed = wide * lax.rsqrt(jnp.mean(wide * wide, axis=-1, keepdims=True) + 1e-05) * gain
    heads = normed.reshape(steps, reqs, kv_heads, group, head)
    query = jnp.transpose(heads.astype(jnp.bfloat16), (1, 2, 0, 3, 4))
    query = query.reshape(reqs, kv_heads, steps * group, head)
    fresh = jnp.mean(heads, axis=3).astype(jnp.bfloat16)
    fresh = jnp.transpose(fresh, (1, 2, 0, 3))
    factor = 1.0 / math.sqrt(head)
    wide_query = jnp.broadcast_to(query[:, None], (reqs, pages) + query.shape[1:])
    cache_scores = (
        jnp.einsum("rjgxd,rjgpd->rjgxp", wide_query, keys, preferred_element_type=jnp.float32)
        * factor
    )
    positions = jnp.arange(pages)[:, None] * page_len + jnp.arange(page_len)[None, :]
    live = positions[None] < lens[:, None, None]
    cache_scores = jnp.where(live[:, :, None, None, :], cache_scores, -1e30)
    new_scores = (
        jnp.einsum("rgxd,rgsd->rgxs", query, fresh, preferred_element_type=jnp.float32) * factor
    )
    step_of = jnp.arange(steps * group) // group
    done = jnp.arange(steps)[None, :] <= step_of[:, None]
    new_scores = jnp.where(done[None, None], new_scores, -1e30)
    top = jnp.maximum(
        jnp.max(cache_scores, axis=(1, 4)), jnp.max(new_scores, axis=-1)
    )[..., None]
    cache_exp = jnp.exp(cache_scores - top[:, None])
    new_exp = jnp.exp(new_scores - top)
    total = jnp.sum(cache_exp, axis=(1, 4))[..., None] + jnp.sum(new_exp, axis=-1, keepdims=True)
    cache_w = (cache_exp / total[:, None]).astype(jnp.bfloat16)
    new_w = (new_exp / total).astype(jnp.bfloat16)
    attended = jnp.einsum(
        "rjgxp,rjgpd->rjgxd", cache_w, values, preferred_element_type=jnp.float32
    ).sum(axis=1)
    attended = attended + jnp.einsum(
        "rgxs,rgsd->rgxd", new_w, fresh, preferred_element_type=jnp.float32
    )
    attended = attended.reshape(reqs, kv_heads, steps, group, head)
    attended = jnp.transpose(attended, (2, 0, 1, 3, 4)).reshape(steps, reqs, width)
    return (wide + scale * attended).astype(jnp.bfloat16)


def copy_kernel(table_ref, page_ref, *refs):
    keys_ref, values_ref = refs[-2], refs[-1]
    keys_ref[0, 0] = page_ref[0, 0]
    values_ref[0, 0] = page_ref[0, 1]


def gather_chunk(pool, table, chunk, block, previous):
    reqs, pages = table.shape
    kv_heads, page_len, head = pool.shape[2:]

    def page_index(r, j, table_ref):
        return (table_ref[(chunk * block + r) * pages + j], 0, 0, 0, 0)

    def slot_index(r, j, table_ref):
        return (chunk * block + r, j, 0, 0, 0)

    slot = pl.BlockSpec((1, 1, kv_heads, page_len, head), slot_index)
    in_specs = [pl.BlockSpec((1, 2, kv_heads, page_len, head), page_index)]
    operands = [table.reshape(-1), pool]
    aliases = {}
    if previous is not None:
        in_specs += [pl.BlockSpec(memory_space=pl.ANY)] * 2
        operands += list(previous)
        aliases = {2: 0, 3: 1}
    grid_spec = pltpu.PrefetchScalarGridSpec(
        num_scalar_prefetch=1,
        grid=(block, pages),
        in_specs=in_specs,
        out_specs=[slot, slot],
    )
    half = jax.ShapeDtypeStruct((reqs, pages, kv_heads, page_len, head), pool.dtype)
    return pl.pallas_call(
        copy_kernel, grid_spec=grid_spec, out_shape=[half, half], input_output_aliases=aliases
    )(*operands)

def per_device(tokens, kv_pool, page_table, lengths, migrate_ids, norm_gain, out_scale):
    inputs = tokens[0]
    pool = kv_pool[0, 0]
    table = page_table[0]
    lens = lengths[0]
    moving = migrate_ids[0]
    gain = norm_gain[0]
    scale = out_scale[0]
    steps, reqs, width = inputs.shape
    page_len = pool.shape[3]
    chosen = table[moving]
    spots = jnp.arange(chosen.shape[1])[:, None] * page_len + jnp.arange(page_len)[None, :]
    arrived_lens = partner(lens[moving], "inst", 0)
    lens_used = lens
    section = lax.axis_index("section")
    count = lax.axis_size("section")
    chunks = CHUNKS
    block = reqs // chunks

    incoming = jnp.zeros((steps, block, width), jnp.bfloat16)
    keys, values = None, None
    results = []
    for k in range(chunks + count - 1):
        if k < chunks:
            previous = None if keys is None else (keys, values)
            keys, values = gather_chunk(pool, table, k, block, previous)
        item = k - section
        start = jnp.clip(item, 0, chunks - 1) * block
        if k == 3:
            start, incoming, chosen = lax.optimization_barrier((start, incoming, chosen))
            received = partner(pool[chosen], "inst", 0)
            keep = spots[None, :, :] < arrived_lens[:, None, None]
            arrived = jnp.where(
                keep[:, :, None, None, :, None], received, jnp.zeros((), jnp.bfloat16)
            )
        elif k > 0:
            start, incoming = lax.optimization_barrier((start, incoming))
        if k == 0:
            rows = inputs[:, :block]
        elif k < chunks:
            first = lax.dynamic_slice_in_dim(inputs, start, block, 1)
            rows = jnp.where(section == 0, first, incoming)
        else:
            rows = incoming
        part_keys = lax.dynamic_slice_in_dim(keys, start, block, 0)
        part_values = lax.dynamic_slice_in_dim(values, start, block, 0)
        part_lens = lax.dynamic_slice_in_dim(lens_used, start, block, 0)
        result = layer(rows, part_keys, part_values, part_lens, gain, scale)
        results.append(result)
        pairs = [(s, s + 1) for s in range(count - 1) if 0 <= k - s < chunks]
        if pairs:
            incoming = lax.ppermute(result, "section", pairs)
    stacked = jnp.stack(results)
    finished = jnp.concatenate(
        [lax.dynamic_index_in_dim(stacked, c + section, 0, False) for c in range(chunks)], axis=1
    )
    handed = partner(finished[:, moving], "inst", 0)
    finished = finished.at[:, moving].set(handed)
    return (finished[None, None], arrived[None, None])


def solution(mesh):
    in_specs = (
        P(("groups", "inst"), None, None, None),
        P(("groups", "inst"), "section", None, None, None, None, None),
        P(("groups", "inst"), None, None),
        P(("groups", "inst"), None),
        P(("groups", "inst"), None),
        P("section", None),
        P("section", None),
    )
    out_specs = (
        P(("groups", "inst"), "section", None, None, None),
        P(("groups", "inst"), "section", None, None, None, None, None, None),
    )
    return jax.shard_map(
        per_device, mesh=mesh, in_specs=in_specs, out_specs=out_specs, check_vma=False
    )
```
